512 devices in a mesh: dp: 4 (over x), tensor: 128 (over y, z, core).
Axes of the slice: x: 4, y: 4, z: 16, core: 2. Of those that a mesh axis runs over, the one named last changes fastest.
Arguments:
- stream: bfloat16 [32768, 2560], P(('dp', 'tensor')), parts along dimension 0, may hold values from -6 to 6
- queries: bfloat16 [512, 2560], P(('dp', 'tensor')), parts along dimension 0, may hold values from -170 to 170
- fresh_entries: bfloat16 [512, 1024], P(('dp', 'tensor')), parts along dimension 0, may hold values from -6 to 6
- paged_store_cache: bfloat16 [2560, 2, 128, 512], P(('dp', 'tensor')), parts along dimension 0, may hold values from -6 to 6
- page_table: int32 [512, 32], P('dp'), parts along dimension 0, may hold values from -1 to 639, as said below
- cache_length: int32 [512], P('dp'), parts along dimension 0, may hold values from 1 to 4096, as said below
- out_proj: bfloat16 [2560, 2560], P(None, 'tensor'), may hold values from -0.125 to 0.125
- norm_gain: bfloat16 [2560], replicated, may hold values from 0.099609375 to 1.8984375
- router: bfloat16 [2560, 64], replicated, may hold values from -0.125 to 0.125
- routes: int32 [32768, 6], P(('dp', 'tensor')), parts along dimension 0, may hold values from 0 to 63, as said below
- gate_up: bfloat16 [2, 24576, 2560], P(None, 'tensor'), may hold values from -0.125 to 0.125
- down_proj: bfloat16 [24576, 2560], P('tensor'), may hold values from -0.15625 to 0.15625
Outputs:
- layer_out: bfloat16 [32768, 2560], P(('dp', 'tensor')), parts along dimension 0
The draws below stay inside these ranges and needn't reach their ends.
There are 4 independent parts, one for each index of `dp`. The reference program is written for one: setup_inputs(seed, part) draws one part's arguments, and reference() takes and returns one part's arrays. A program takes and returns all parts, laid end to end along the dimension named above; an argument that names none is the same for every part. Nothing has to cross between parts.
Inputs may be any that keep to these rules, and one draw needn't show every extreme that they name: `routes`: each row names 6 different experts. The rows of one device name each expert at most 6 times, and on every device one and the same expert below 16 is named exactly 6 times. `page_table`: row r lists in order the pages of request r's cache, ceil(cache_length[r] / 128) of them, then -1; every page belongs to exactly one request. `cache_length`: some request's cache holds exactly 4096 tokens.
All inputs are finite; a program needn't handle non-finite values.
Results may differ from the reference program's by a relative error of at most 0.0045.
Values may be sent and summed in bfloat16 or wider, within the bound.
No kernel may reach another device: no remote copies, remote signals or barrier semaphores. Data moves between devices by JAX's collectives and lax.ppermute only.
A program may use at most 64 MiB of HBM per device.

```python
import math
import jax
import jax.numpy as jnp
from jax import lax

D = 2560
QUERY_HEADS = 20
KEY_VALUE_HEADS = 4
HEAD_SIZE = 128
EXPERTS_ALL = 64
EXPERT_FF = 1536
TOPK = 6
GROUP = 8
DEC_DEV = 1
PAGE_TOKENS = 128
LONGEST_PAGES = 32
TOK_DEV = 64
HID_DEV = 192
EXP = 16
CAP = 6
TOKENS = 8192
DECODE_REQUESTS = 128
CACHE_PAGES = 640
N_TENSOR = 128


def draw_queries(key, part):
    attention_result = jax.random.truncated_normal(jax.random.fold_in(key, 103), -6.0, 6.0, (DECODE_REQUESTS, QUERY_HEADS * HEAD_SIZE), jnp.float32)
    return attention_result.astype(jnp.bfloat16)


def draw_fresh_entries(key, part):
    attention_result = jax.random.truncated_normal(jax.random.fold_in(key, 111), -6.0, 6.0, (DECODE_REQUESTS, 2 * KEY_VALUE_HEADS * HEAD_SIZE), jnp.float32)
    return attention_result.astype(jnp.bfloat16)


def draw_paged_store_cache(key, part):
    attention_result = jax.random.truncated_normal(jax.random.fold_in(key, 121), -6.0, 6.0, (CACHE_PAGES, 2, PAGE_TOKENS, KEY_VALUE_HEADS * HEAD_SIZE), jnp.float32)
    return attention_result.astype(jnp.bfloat16)


def page_layout(key):
    key_grid = jax.random.fold_in(key, 201)
    key_long = jax.random.fold_in(key, 202)
    key_perm = jax.random.fold_in(key, 203)
    key_fill = jax.random.fold_in(key, 204)
    spare = CACHE_PAGES - LONGEST_PAGES - (DECODE_REQUESTS - 1)
    grid = jax.random.permutation(key_grid, (DECODE_REQUESTS - 1) * (LONGEST_PAGES - 1)).reshape(DECODE_REQUESTS - 1, LONGEST_PAGES - 1)
    others = 1 + jnp.sum((grid < spare).astype(jnp.int32), axis=1)
    longest = jax.random.randint(key_long, (), 0, DECODE_REQUESTS)
    order = jnp.arange(DECODE_REQUESTS, dtype=jnp.int32)
    source = jnp.clip(order - (order > longest).astype(jnp.int32), 0, DECODE_REQUESTS - 2)
    counts = jnp.where(order == longest, LONGEST_PAGES, others[source])
    starts = jnp.cumsum(counts) - counts
    shuffled = jax.random.permutation(key_perm, CACHE_PAGES).astype(jnp.int32)
    slots = jnp.arange(LONGEST_PAGES, dtype=jnp.int32)
    flat = jnp.clip(starts[:, None] + slots[None, :], 0, CACHE_PAGES - 1)
    table = jnp.where(slots[None, :] < counts[:, None], shuffled[flat], -1)
    filled = jax.random.randint(key_fill, (DECODE_REQUESTS,), 1, PAGE_TOKENS + 1)
    filled = jnp.where(order == longest, PAGE_TOKENS, filled)
    lengths = (counts - 1) * PAGE_TOKENS + filled
    return (table.astype(jnp.int32), lengths.astype(jnp.int32))


def draw_page_table(key, part):
    return page_layout(key)[0]


def draw_cache_length(key, part):
    return page_layout(key)[1]


def draw_routes(key, part):
    blocks = TOKENS // TOK_DEV
    target = jax.random.randint(jax.random.fold_in(key, 301), (), 0, EXP)
    block_keys = jax.random.split(jax.random.fold_in(key, 302), blocks)
    orders = jax.vmap(lambda block_key: jax.random.permutation(block_key, EXPERTS_ALL))(block_keys).astype(jnp.int32)
    place = jnp.sum(jnp.where(orders == target, jnp.arange(EXPERTS_ALL, dtype=jnp.int32)[None, :], 0), axis=1)
    remain = TOK_DEV % EXPERTS_ALL
    if remain > 0:
        offset = TOPK - 1 + jax.random.randint(jax.random.fold_in(key, 303), (blocks,), 0, remain - TOPK + 1)
    else:
        offset = jax.random.randint(jax.random.fold_in(key, 303), (blocks,), 0, EXPERTS_ALL)
    begin = jnp.mod(place - offset, EXPERTS_ALL)
    rows = jnp.arange(TOK_DEV, dtype=jnp.int32)
    picks = jnp.arange(TOPK, dtype=jnp.int32)
    spots = jnp.mod(begin[:, None, None] + rows[None, :, None] + picks[None, None, :], EXPERTS_ALL)
    spread_orders = jnp.broadcast_to(orders[:, None, :], (blocks, TOK_DEV, EXPERTS_ALL))
    chosen = jnp.take_along_axis(spread_orders, spots, axis=2)
    return chosen.reshape(TOKENS, TOPK).astype(jnp.int32)


def block_scale(key, extent, cuts, low, top_value):
    loudness, own = 1.0, jax.random.fold_in(key, 6)
    for dim, parts in cuts:
        draws = jnp.exp(jax.random.uniform(jax.random.fold_in(own, dim), (parts,), jnp.float32, low / len(cuts), top_value / len(cuts)))
        loudness = loudness * jnp.repeat(draws, extent[dim] // parts).reshape([-1 if axis == dim else 1 for axis in range(len(extent))])
    return loudness


def normal_values(stream_key, extent, deviation, bound, shards=(), kind=jnp.bfloat16):
    array = deviation * jax.random.normal(stream_key, extent, jnp.float32)
    if shards:
        array = array * block_scale(stream_key, extent, shards, -0.22, 0.18)
    return jnp.clip(array, -bound, bound).astype(kind)


def setup_inputs(seed: int = 0, part: int = 0) -> dict:
    streams_of = jax.random.split(jax.random.key(seed), 13)
    part_keys = jax.random.split(jax.random.fold_in(streams_of[12], part), 13)
    stream = normal_values(part_keys[0], (TOKENS, D), 1.0, 6.0, ((0, 128),))
    queries = draw_queries(jax.random.fold_in(jax.random.fold_in(streams_of[12], part), 71), part)
    fresh_entries = draw_fresh_entries(jax.random.fold_in(jax.random.fold_in(streams_of[12], part), 71), part)
    paged_store_cache = draw_paged_store_cache(jax.random.fold_in(jax.random.fold_in(streams_of[12], part), 71), part)
    page_table = draw_page_table(jax.random.fold_in(jax.random.fold_in(streams_of[12], part), 71), part)
    cache_length = draw_cache_length(jax.random.fold_in(jax.random.fold_in(streams_of[12], part), 71), part)
    out_proj = normal_values(streams_of[6], (QUERY_HEADS * HEAD_SIZE, D), (QUERY_HEADS * HEAD_SIZE) ** -0.5, 0.125, ((1, 128),))
    norm_gain = jnp.clip(1.0 + 0.18 * jax.random.normal(streams_of[7], (D,), jnp.float32), 0.099609375, 1.8984375).astype(jnp.bfloat16)
    router = normal_values(streams_of[8], (D, EXPERTS_ALL), D ** -0.5, 0.125)
    routes = draw_routes(jax.random.fold_in(jax.random.fold_in(streams_of[12], part), 71), part)
    gate_up = normal_values(streams_of[10], (2, EXP * EXPERT_FF, D), D ** -0.5, 0.125, ((1, 128),))
    down_proj = normal_values(streams_of[11], (EXP * EXPERT_FF, D), EXPERT_FF ** -0.5, 0.15625, ((0, 128),))
    return dict(stream=stream, queries=queries, fresh_entries=fresh_entries, paged_store_cache=paged_store_cache, page_table=page_table, cache_length=cache_length, out_proj=out_proj, norm_gain=norm_gain, router=router, routes=routes, gate_up=gate_up, down_proj=down_proj)


NEG_FILL = -1e+30
EPSILON = 1e-05

def reference(stream, queries, fresh_entries, paged_store_cache, page_table, cache_length, out_proj, norm_gain, router, routes, gate_up, down_proj):
    query_groups = QUERY_HEADS // KEY_VALUE_HEADS
    key_value_width = KEY_VALUE_HEADS * HEAD_SIZE
    score_scale = 1.0 / math.sqrt(HEAD_SIZE)
    positions = jnp.arange(LONGEST_PAGES * PAGE_TOKENS, dtype=jnp.int32)

    def attend(request_index):
        query_vector = queries[request_index].astype(jnp.float32).reshape(KEY_VALUE_HEADS, query_groups, HEAD_SIZE)
        page_ids = jnp.maximum(page_table[request_index], 0)
        page_tile_block = paged_store_cache[page_ids]
        key_matrix = page_tile_block[:, 0].reshape(LONGEST_PAGES * PAGE_TOKENS, KEY_VALUE_HEADS, HEAD_SIZE).astype(jnp.float32)
        value_matrix = page_tile_block[:, 1].reshape(LONGEST_PAGES * PAGE_TOKENS, KEY_VALUE_HEADS, HEAD_SIZE).astype(jnp.float32)
        scores = jnp.einsum('hgd,thd->hgt', query_vector, key_matrix) * score_scale
        scores = jnp.where(positions[None, None, :] < cache_length[request_index], scores, NEG_FILL)
        token_key = fresh_entries[request_index, :key_value_width].astype(jnp.float32).reshape(KEY_VALUE_HEADS, HEAD_SIZE)
        token_value = fresh_entries[request_index, key_value_width:].astype(jnp.float32).reshape(KEY_VALUE_HEADS, HEAD_SIZE)
        own_score = jnp.einsum('hgd,hd->hg', query_vector, token_key) * score_scale
        maxima = jnp.maximum(lax.optimization_barrier(jnp.max(scores, axis=-1)), own_score)
        weights = jnp.exp(scores - maxima[..., None])
        own_weight = jnp.exp(own_score - maxima)
        totals = lax.optimization_barrier(jnp.sum(weights, axis=-1)) + own_weight
        mixture = jnp.einsum('hgt,thd->hgd', weights, value_matrix) + own_weight[..., None] * token_value[:, None, :]
        return (mixture / totals[..., None]).reshape(QUERY_HEADS * HEAD_SIZE)
    context = lax.map(attend, jnp.arange(DECODE_REQUESTS, dtype=jnp.int32)).astype(jnp.bfloat16)
    projected = jnp.dot(context, out_proj, preferred_element_type=jnp.float32)
    blocks = stream.reshape(N_TENSOR, TOK_DEV, D).astype(jnp.float32)
    blocks = blocks.at[:, :DEC_DEV].add(projected.reshape(N_TENSOR, DEC_DEV, D))
    resid = lax.optimization_barrier(blocks.reshape(TOKENS, D).astype(jnp.bfloat16))
    widened = resid.astype(jnp.float32)
    inverse = lax.rsqrt(lax.optimization_barrier(jnp.mean(widened * widened, axis=-1, keepdims=True)) + EPSILON)
    normed = (widened * inverse * norm_gain.astype(jnp.float32)).astype(jnp.bfloat16)
    logits = jnp.dot(normed, router, preferred_element_type=jnp.float32)
    chosen = jnp.take_along_axis(logits, routes, axis=1)
    gate_probs = jax.nn.softmax(chosen, axis=-1)
    capacity_all = N_TENSOR * CAP
    zero_index = jnp.zeros((), jnp.int32)

    def expert_step(accumulated, expert):
        matched = routes == expert
        routed = jnp.any(matched, axis=1)
        weight_row = lax.optimization_barrier(jnp.sum(jnp.where(matched, gate_probs, 0.0), axis=1))
        picked = jnp.nonzero(routed, size=capacity_all, fill_value=0)[0].astype(jnp.int32)
        alive_rows = (jnp.arange(capacity_all, dtype=jnp.int32) < jnp.sum(routed.astype(jnp.int32))).astype(jnp.float32)
        inputs = normed[picked]
        row_first = (expert * EXPERT_FF).astype(jnp.int32)
        weights_in = lax.dynamic_slice(gate_up, (zero_index, row_first, zero_index), (2, EXPERT_FF, D))
        gate_part = jnp.dot(inputs, weights_in[0].T, preferred_element_type=jnp.float32)
        upward = jnp.dot(inputs, weights_in[1].T, preferred_element_type=jnp.float32)
        active = (jax.nn.silu(gate_part) * upward).astype(jnp.bfloat16)
        weights_out = lax.dynamic_slice(down_proj, (row_first, zero_index), (EXPERT_FF, D))
        summed = jnp.zeros((capacity_all, D), jnp.float32)
        for slice_index in range(GROUP):
            row_start = slice_index * HID_DEV
            partial_value = jnp.dot(active[:, row_start:row_start + HID_DEV], weights_out[row_start:row_start + HID_DEV], preferred_element_type=jnp.float32).astype(jnp.bfloat16)
            summed = summed + partial_value.astype(jnp.float32)
        weighted = summed * (weight_row[picked] * alive_rows)[:, None]
        return (accumulated.at[picked].add(weighted), None)
    routed_sum, _ = lax.scan(expert_step, jnp.zeros((TOKENS, D), jnp.float32), jnp.arange(EXP, dtype=jnp.int32))
    return (widened + routed_sum).astype(jnp.bfloat16)
```

```python
import math

import jax
import jax.numpy as jnp
import numpy as np
from jax import lax
from jax.sharding import Mesh
from jax.sharding import PartitionSpec as P

QUERY_HEADS = 20
KEY_VALUE_HEADS = 4
HEAD_SIZE = 128
GROUP = 8
CAP = 6


NEG_FILL = -1e30
EPSILON = 1e-05

TENSOR = ("y", "zh", "zl", "c")


def gather_nested(x):
    x = lax.all_gather(x, "c", axis=0, tiled=True)
    x = lax.all_gather(x, ("zh", "zl"), axis=0, tiled=True)
    return lax.all_gather(x, "y", axis=0, tiled=True)


def local_parts(query_all, paged_store_cache, page_table, cache_length, my_index):
    request_page_count = paged_store_cache.shape[0]
    page_length = paged_store_cache.shape[2]
    longest = page_table.shape[1]
    query_groups = QUERY_HEADS // KEY_VALUE_HEADS
    global_ids = my_index * request_page_count + jnp.arange(request_page_count, dtype=jnp.int32)
    matched = page_table[None, :, :] == global_ids[:, None, None]
    owner = jnp.any(matched, axis=2)
    position = jnp.sum(
        jnp.where(matched, jnp.arange(longest, dtype=jnp.int32)[None, None, :], 0), axis=(1, 2)
    )
    length_here = jnp.sum(jnp.where(owner, cache_length[None, :], 0), axis=1)
    query_page_scores = jnp.dot(
        owner.astype(jnp.bfloat16), query_all, preferred_element_type=jnp.float32
    ).astype(jnp.bfloat16)
    query_page_scores = query_page_scores.reshape(
        request_page_count, KEY_VALUE_HEADS, query_groups, HEAD_SIZE
    )
    key_matrix = paged_store_cache[:, 0].reshape(
        request_page_count, page_length, KEY_VALUE_HEADS, HEAD_SIZE
    )
    value_matrix = (
        paged_store_cache[:, 1]
        .reshape(request_page_count, page_length, KEY_VALUE_HEADS, HEAD_SIZE)
        .astype(jnp.float32)
    )
    scores = jnp.einsum(
        "phgd,pthd->phgt", query_page_scores, key_matrix, preferred_element_type=jnp.float32
    ) * (1.0 / math.sqrt(HEAD_SIZE))
    offsets = jnp.arange(page_length, dtype=jnp.int32)
    valid = position[:, None] * page_length + offsets[None, :] < length_here[:, None]
    scores = jnp.where(valid[:, None, None, :], scores, NEG_FILL)
    page_max = jnp.max(scores, axis=-1)
    weights = jnp.exp(scores - page_max[..., None])
    page_total = jnp.sum(weights, axis=-1)
    page_accum = jnp.einsum("phgt,pthd->phgd", weights, value_matrix)
    owned = owner[:, :, None, None]
    request_max = jnp.max(jnp.where(owned, page_max[:, None], NEG_FILL), axis=0)
    coef = jnp.where(owned, jnp.exp(page_max[:, None] - request_max[None]), 0.0)
    request_total = jnp.sum(coef * page_total[:, None], axis=0)
    request_accum = jnp.einsum("prhg,phgd->rhgd", coef, page_accum)
    return (request_max, request_total, request_accum)


def finish_context(parts, local_queries, local_entries):
    entry_count = local_queries.shape[0]
    key_value_width = KEY_VALUE_HEADS * HEAD_SIZE
    query_vector = local_queries.reshape(
        entry_count, KEY_VALUE_HEADS, QUERY_HEADS // KEY_VALUE_HEADS, HEAD_SIZE
    )
    token_key = local_entries[:, :key_value_width].reshape(entry_count, KEY_VALUE_HEADS, HEAD_SIZE)
    token_value = (
        local_entries[:, key_value_width:]
        .reshape(entry_count, KEY_VALUE_HEADS, HEAD_SIZE)
        .astype(jnp.float32)
    )
    own_score = jnp.einsum(
        "rhgd,rhd->rhg", query_vector, token_key, preferred_element_type=jnp.float32
    ) * (1.0 / math.sqrt(HEAD_SIZE))
    part_max = parts[..., 0]
    part_total = parts[..., 1]
    part_accum = parts[..., 2:]
    joined = jnp.maximum(jnp.max(part_max, axis=1), own_score)
    coef = jnp.exp(part_max - joined[:, None])
    own_weight = jnp.exp(own_score - joined)
    totals = jnp.sum(coef * part_total, axis=1) + own_weight
    accum = (
        jnp.sum(coef[..., None] * part_accum, axis=1)
        + own_weight[..., None] * token_value[:, :, None, :]
    )
    return (
        (accum / totals[..., None])
        .reshape(entry_count, QUERY_HEADS * HEAD_SIZE)
        .astype(jnp.bfloat16)
    )


def local(
    stream,
    queries,
    fresh_entries,
    paged_store_cache,
    page_table,
    cache_length,
    out_proj,
    norm_gain,
    router,
    routes,
    gate_up,
    down_proj,
):
    tensor_count = lax.axis_size(TENSOR)
    my_index = lax.axis_index(TENSOR)
    dec_rows = queries.shape[0]
    query_all = gather_nested(queries)
    request_max, request_total, request_accum = local_parts(
        query_all, paged_store_cache, page_table, cache_length, my_index
    )
    packed = jnp.concatenate(
        (request_max[..., None], request_total[..., None], request_accum), axis=-1
    )
    packed = packed.reshape((tensor_count, dec_rows) + packed.shape[1:])
    parts = lax.all_to_all(packed, TENSOR, split_axis=0, concat_axis=0, tiled=True)
    parts = jnp.swapaxes(parts, 0, 1)
    context = finish_context(parts, queries, fresh_entries)
    context_all = gather_nested(context)
    projected = jnp.dot(context_all, out_proj, preferred_element_type=jnp.float32)
    column_block = projected.shape[1]
    arrived = lax.all_to_all(
        projected.reshape(tensor_count, dec_rows, column_block),
        TENSOR,
        split_axis=0,
        concat_axis=2,
        tiled=True,
    )
    widened = stream.astype(jnp.float32)
    widened = widened.at[:dec_rows].add(arrived[0])
    resid = lax.optimization_barrier(widened.astype(jnp.bfloat16))
    widened = resid.astype(jnp.float32)
    inverse = lax.rsqrt(jnp.mean(widened * widened, axis=-1, keepdims=True) + EPSILON)
    normed = (widened * inverse * norm_gain.astype(jnp.float32)).astype(jnp.bfloat16)
    logits = jnp.dot(normed, router, preferred_element_type=jnp.float32)
    chosen = jnp.take_along_axis(logits, routes, axis=1)
    gate_probs = jax.nn.softmax(chosen, axis=-1)
    expert_count = tensor_count // GROUP
    expert_ids = jnp.arange(expert_count, dtype=jnp.int32)
    matched = routes[:, :, None] == expert_ids[None, None, :]
    routed = jnp.any(matched, axis=1)
    gate_weight = jnp.sum(jnp.where(matched, gate_probs[:, :, None], 0.0), axis=1)
    routed_count = routed.astype(jnp.int32)
    ranking = jnp.cumsum(routed_count, axis=0) - routed_count
    slot_ids = jnp.arange(CAP, dtype=jnp.int32)
    selector = routed.T[:, None, :] & (ranking.T[:, None, :] == slot_ids[None, :, None])
    slot_rows = jnp.einsum(
        "eci,id->ecd", selector.astype(jnp.bfloat16), normed, preferred_element_type=jnp.float32
    ).astype(jnp.bfloat16)
    outgoing = jnp.repeat(slot_rows, GROUP, axis=0)
    contract_last = (((1,), (1,)), ((), ()))
    incoming = lax.all_to_all(outgoing, TENSOR, split_axis=0, concat_axis=0, tiled=True)
    shape_in = incoming.shape
    flat_rows = incoming.reshape(-1, shape_in[2])
    gate_part = lax.dot_general(
        flat_rows, gate_up[0], contract_last, preferred_element_type=jnp.float32
    )
    upward = lax.dot_general(
        flat_rows, gate_up[1], contract_last, preferred_element_type=jnp.float32
    )
    active = (jax.nn.silu(gate_part) * upward).astype(jnp.bfloat16)
    partial_value = jnp.dot(active, down_proj, preferred_element_type=jnp.float32).astype(
        jnp.bfloat16
    )
    returned = lax.all_to_all(
        partial_value.reshape(shape_in), TENSOR, split_axis=0, concat_axis=0, tiled=True
    )
    expert_out = jnp.sum(
        returned.reshape(expert_count, GROUP, CAP, returned.shape[2]), axis=1, dtype=jnp.float32
    )
    weighted = selector.astype(jnp.float32) * gate_weight.T[:, None, :]
    routed_sum = jnp.einsum("eci,ecd->id", weighted, expert_out)
    return (widened + routed_sum).astype(jnp.bfloat16)


def physical_mesh(mesh):
    dp_count, tensor_count = mesh.devices.shape
    z_count = tensor_count // 2 // 4
    z_low = 4 if z_count % 4 == 0 else z_count
    shape = (dp_count, 4, z_count // z_low, z_low, 2)
    return Mesh(np.asarray(mesh.devices).reshape(shape), ("dp",) + TENSOR)


def solution(mesh):
    mesh = physical_mesh(mesh)
    rows = ("dp",) + TENSOR
    placed = (
        P(rows, None),
        P(rows, None),
        P(rows, None),
        P(rows, None, None, None),
        P("dp", None),
        P("dp"),
        P(None, TENSOR),
        P(),
        P(),
        P(rows, None),
        P(None, TENSOR, None),
        P(TENSOR, None),
    )
    return jax.shard_map(
        local, mesh=mesh, in_specs=placed, out_specs=P(rows, None), check_vma=False
    )
```

```python
import math

import jax
import jax.numpy as jnp
import numpy as np
from jax import lax
from jax.sharding import Mesh
from jax.sharding import PartitionSpec as P

QUERY_HEADS = 20
KEY_VALUE_HEADS = 4
HEAD_SIZE = 128
GROUP = 8
CAP = 6


NEG_FILL = -1e30
EPSILON = 1e-05

TENSOR = ("y", "zh", "zl", "c")
EXPERT_AXES = ("y", "zh")
SLICE_AXES = ("zl", "c")


def gather_nested(x):
    x = lax.all_gather(x, "c", axis=0, tiled=True)
    x = lax.all_gather(x, ("zh", "zl"), axis=0, tiled=True)
    return lax.all_gather(x, "y", axis=0, tiled=True)


def local_parts(query_all, paged_store_cache, page_table, cache_length, my_index):
    request_page_count = paged_store_cache.shape[0]
    page_length = paged_store_cache.shape[2]
    longest = page_table.shape[1]
    query_groups = QUERY_HEADS // KEY_VALUE_HEADS
    global_ids = my_index * request_page_count + jnp.arange(request_page_count, dtype=jnp.int32)
    matched = page_table[None, :, :] == global_ids[:, None, None]
    owner = jnp.any(matched, axis=2)
    position = jnp.sum(
        jnp.where(matched, jnp.arange(longest, dtype=jnp.int32)[None, None, :], 0), axis=(1, 2)
    )
    length_here = jnp.sum(jnp.where(owner, cache_length[None, :], 0), axis=1)
    query_page_scores = jnp.dot(
        owner.astype(jnp.bfloat16), query_all, preferred_element_type=jnp.float32
    ).astype(jnp.bfloat16)
    query_page_scores = query_page_scores.reshape(
        request_page_count, KEY_VALUE_HEADS, query_groups, HEAD_SIZE
    )
    key_matrix = paged_store_cache[:, 0].reshape(
        request_page_count, page_length, KEY_VALUE_HEADS, HEAD_SIZE
    )
    value_matrix = (
        paged_store_cache[:, 1]
        .reshape(request_page_count, page_length, KEY_VALUE_HEADS, HEAD_SIZE)
        .astype(jnp.float32)
    )
    scores = jnp.einsum(
        "phgd,pthd->phgt", query_page_scores, key_matrix, preferred_element_type=jnp.float32
    ) * (1.0 / math.sqrt(HEAD_SIZE))
    offsets = jnp.arange(page_length, dtype=jnp.int32)
    valid = position[:, None] * page_length + offsets[None, :] < length_here[:, None]
    scores = jnp.where(valid[:, None, None, :], scores, NEG_FILL)
    page_max = jnp.max(scores, axis=-1)
    weights = jnp.exp(scores - page_max[..., None])
    page_total = jnp.sum(weights, axis=-1)
    page_accum = jnp.einsum("phgt,pthd->phgd", weights, value_matrix)
    owned = owner[:, :, None, None]
    request_max = jnp.max(jnp.where(owned, page_max[:, None], NEG_FILL), axis=0)
    coef = jnp.where(owned, jnp.exp(page_max[:, None] - request_max[None]), 0.0)
    request_total = jnp.sum(coef * page_total[:, None], axis=0)
    request_accum = jnp.einsum("prhg,phgd->rhgd", coef, page_accum)
    return (request_max, request_total, request_accum)


def finish_context(parts, local_queries, local_entries):
    entry_count = local_queries.shape[0]
    key_value_width = KEY_VALUE_HEADS * HEAD_SIZE
    query_vector = local_queries.reshape(
        entry_count, KEY_VALUE_HEADS, QUERY_HEADS // KEY_VALUE_HEADS, HEAD_SIZE
    )
    token_key = local_entries[:, :key_value_width].reshape(entry_count, KEY_VALUE_HEADS, HEAD_SIZE)
    token_value = (
        local_entries[:, key_value_width:]
        .reshape(entry_count, KEY_VALUE_HEADS, HEAD_SIZE)
        .astype(jnp.float32)
    )
    own_score = jnp.einsum(
        "rhgd,rhd->rhg", query_vector, token_key, preferred_element_type=jnp.float32
    ) * (1.0 / math.sqrt(HEAD_SIZE))
    part_max = parts[..., 0]
    part_total = parts[..., 1]
    part_accum = parts[..., 2:]
    joined = jnp.maximum(jnp.max(part_max, axis=1), own_score)
    coef = jnp.exp(part_max - joined[:, None])
    own_weight = jnp.exp(own_score - joined)
    totals = jnp.sum(coef * part_total, axis=1) + own_weight
    accum = (
        jnp.sum(coef[..., None] * part_accum, axis=1)
        + own_weight[..., None] * token_value[:, :, None, :]
    )
    return (
        (accum / totals[..., None])
        .reshape(entry_count, QUERY_HEADS * HEAD_SIZE)
        .astype(jnp.bfloat16)
    )


def local(
    stream,
    queries,
    fresh_entries,
    paged_store_cache,
    page_table,
    cache_length,
    out_proj,
    norm_gain,
    router,
    routes,
    gate_up,
    down_proj,
):
    tensor_count = lax.axis_size(TENSOR)
    my_index = lax.axis_index(TENSOR)
    dec_rows = queries.shape[0]
    query_all = gather_nested(queries)
    request_max, request_total, request_accum = local_parts(
        query_all, paged_store_cache, page_table, cache_length, my_index
    )
    packed = jnp.concatenate(
        (request_max[..., None], request_total[..., None], request_accum), axis=-1
    )
    packed = packed.reshape((tensor_count, dec_rows) + packed.shape[1:])
    parts = lax.all_to_all(packed, TENSOR, split_axis=0, concat_axis=0, tiled=True)
    parts = jnp.swapaxes(parts, 0, 1)
    context = finish_context(parts, queries, fresh_entries)
    context_all = gather_nested(context)
    projected = jnp.dot(context_all, out_proj, preferred_element_type=jnp.float32)
    column_block = projected.shape[1]
    arrived = lax.all_to_all(
        projected.reshape(tensor_count, dec_rows, column_block),
        TENSOR,
        split_axis=0,
        concat_axis=2,
        tiled=True,
    )
    widened = stream.astype(jnp.float32)
    widened = widened.at[:dec_rows].add(arrived[0])
    resid = lax.optimization_barrier(widened.astype(jnp.bfloat16))
    widened = resid.astype(jnp.float32)
    inverse = lax.rsqrt(jnp.mean(widened * widened, axis=-1, keepdims=True) + EPSILON)
    normed = (widened * inverse * norm_gain.astype(jnp.float32)).astype(jnp.bfloat16)
    logits = jnp.dot(normed, router, preferred_element_type=jnp.float32)
    chosen = jnp.take_along_axis(logits, routes, axis=1)
    gate_probs = jax.nn.softmax(chosen, axis=-1)
    expert_count = tensor_count // GROUP
    expert_ids = jnp.arange(expert_count, dtype=jnp.int32)
    matched = routes[:, :, None] == expert_ids[None, None, :]
    routed = jnp.any(matched, axis=1)
    gate_weight = jnp.sum(jnp.where(matched, gate_probs[:, :, None], 0.0), axis=1)
    routed_count = routed.astype(jnp.int32)
    ranking = jnp.cumsum(routed_count, axis=0) - routed_count
    slot_ids = jnp.arange(CAP, dtype=jnp.int32)
    selector = routed.T[:, None, :] & (ranking.T[:, None, :] == slot_ids[None, :, None])
    slot_rows = jnp.einsum(
        "eci,id->ecd", selector.astype(jnp.bfloat16), normed, preferred_element_type=jnp.float32
    ).astype(jnp.bfloat16)
    contract_last = (((1,), (1,)), ((), ()))
    landed = lax.all_to_all(slot_rows, EXPERT_AXES, split_axis=0, concat_axis=0, tiled=True)
    gathered = lax.all_gather(lax.all_gather(landed, "c", axis=0), "zl", axis=0)
    shape_in = gathered.shape
    flat_rows = gathered.reshape(-1, shape_in[-1])
    gate_part = lax.dot_general(
        flat_rows, gate_up[0], contract_last, preferred_element_type=jnp.float32
    )
    upward = lax.dot_general(
        flat_rows, gate_up[1], contract_last, preferred_element_type=jnp.float32
    )
    active = (jax.nn.silu(gate_part) * upward).astype(jnp.bfloat16)
    partial_value = jnp.dot(active, down_proj, preferred_element_type=jnp.float32).astype(
        jnp.bfloat16
    )
    group_rows = partial_value.astype(jnp.float32).reshape(
        (GROUP,) + landed.shape
    )
    summed = lax.psum_scatter(group_rows, SLICE_AXES, scatter_dimension=0, tiled=True)
    expert_out = lax.all_to_all(
        summed.reshape(landed.shape), EXPERT_AXES, split_axis=0, concat_axis=0, tiled=True
    )
    weighted = selector.astype(jnp.float32) * gate_weight.T[:, None, :]
    routed_sum = jnp.einsum("eci,ecd->id", weighted, expert_out)
    return (widened + routed_sum).astype(jnp.bfloat16)


def physical_mesh(mesh):
    dp_count, tensor_count = mesh.devices.shape
    z_count = tensor_count // 2 // 4
    z_low = GROUP // 2
    shape = (dp_count, 4, z_count // z_low, z_low, 2)
    return Mesh(np.asarray(mesh.devices).reshape(shape), ("dp",) + TENSOR)


def solution(mesh):
    mesh = physical_mesh(mesh)
    rows = ("dp",) + TENSOR
    placed = (
        P(rows, None),
        P(rows, None),
        P(rows, None),
        P(rows, None, None, None),
        P("dp", None),
        P("dp"),
        P(None, TENSOR),
        P(),
        P(),
        P(rows, None),
        P(None, TENSOR, None),
        P(TENSOR, None),
    )
    return jax.shard_map(
        local, mesh=mesh, in_specs=placed, out_specs=P(rows, None), check_vma=False
    )
```

```python
import math

import jax
import jax.numpy as jnp
import numpy as np
from jax import lax
from jax.sharding import Mesh
from jax.sharding import PartitionSpec as P

QUERY_HEADS = 20
KEY_VALUE_HEADS = 4
HEAD_SIZE = 128
GROUP = 8
CAP = 6


NEG_FILL = -1e30
EPSILON = 1e-05

TENSOR = ("y", "zh", "zl", "c")
EXPERT_AXES = ("y", "zh")


def gather_nested(x):
    x = lax.all_gather(x, "c", axis=0, tiled=True)
    x = lax.all_gather(x, ("zh", "zl"), axis=0, tiled=True)
    return lax.all_gather(x, "y", axis=0, tiled=True)


def local_parts(query_all, paged_store_cache, page_table, cache_length, my_index):
    request_page_count = paged_store_cache.shape[0]
    page_length = paged_store_cache.shape[2]
    longest = page_table.shape[1]
    query_groups = QUERY_HEADS // KEY_VALUE_HEADS
    global_ids = my_index * request_page_count + jnp.arange(request_page_count, dtype=jnp.int32)
    matched = page_table[None, :, :] == global_ids[:, None, None]
    owner = jnp.any(matched, axis=2)
    position = jnp.sum(
        jnp.where(matched, jnp.arange(longest, dtype=jnp.int32)[None, None, :], 0), axis=(1, 2)
    )
    length_here = jnp.sum(jnp.where(owner, cache_length[None, :], 0), axis=1)
    query_page_scores = jnp.dot(
        owner.astype(jnp.bfloat16), query_all, preferred_element_type=jnp.float32
    ).astype(jnp.bfloat16)
    query_page_scores = query_page_scores.reshape(
        request_page_count, KEY_VALUE_HEADS, query_groups, HEAD_SIZE
    )
    key_matrix = paged_store_cache[:, 0].reshape(
        request_page_count, page_length, KEY_VALUE_HEADS, HEAD_SIZE
    )
    value_matrix = (
        paged_store_cache[:, 1]
        .reshape(request_page_count, page_length, KEY_VALUE_HEADS, HEAD_SIZE)
        .astype(jnp.float32)
    )
    scores = jnp.einsum(
        "phgd,pthd->phgt", query_page_scores, key_matrix, preferred_element_type=jnp.float32
    ) * (1.0 / math.sqrt(HEAD_SIZE))
    offsets = jnp.arange(page_length, dtype=jnp.int32)
    valid = position[:, None] * page_length + offsets[None, :] < length_here[:, None]
    scores = jnp.where(valid[:, None, None, :], scores, NEG_FILL)
    page_max = jnp.max(scores, axis=-1)
    weights = jnp.exp(scores - page_max[..., None])
    page_total = jnp.sum(weights, axis=-1)
    page_accum = jnp.einsum("phgt,pthd->phgd", weights, value_matrix)
    owned = owner[:, :, None, None]
    request_max = jnp.max(jnp.where(owned, page_max[:, None], NEG_FILL), axis=0)
    coef = jnp.where(owned, jnp.exp(page_max[:, None] - request_max[None]), 0.0)
    request_total = jnp.sum(coef * page_total[:, None], axis=0)
    request_accum = jnp.einsum("prhg,phgd->rhgd", coef, page_accum)
    return (request_max, request_total, request_accum)


def finish_context(parts, local_queries, local_entries):
    entry_count = local_queries.shape[0]
    key_value_width = KEY_VALUE_HEADS * HEAD_SIZE
    query_vector = local_queries.reshape(
        entry_count, KEY_VALUE_HEADS, QUERY_HEADS // KEY_VALUE_HEADS, HEAD_SIZE
    )
    token_key = local_entries[:, :key_value_width].reshape(entry_count, KEY_VALUE_HEADS, HEAD_SIZE)
    token_value = (
        local_entries[:, key_value_width:]
        .reshape(entry_count, KEY_VALUE_HEADS, HEAD_SIZE)
        .astype(jnp.float32)
    )
    own_score = jnp.einsum(
        "rhgd,rhd->rhg", query_vector, token_key, preferred_element_type=jnp.float32
    ) * (1.0 / math.sqrt(HEAD_SIZE))
    part_max = parts[..., 0]
    part_total = parts[..., 1]
    part_accum = parts[..., 2:]
    joined = jnp.maximum(jnp.max(part_max, axis=1), own_score)
    coef = jnp.exp(part_max - joined[:, None])
    own_weight = jnp.exp(own_score - joined)
    totals = jnp.sum(coef * part_total, axis=1) + own_weight
    accum = (
        jnp.sum(coef[..., None] * part_accum, axis=1)
        + own_weight[..., None] * token_value[:, :, None, :]
    )
    return (
        (accum / totals[..., None])
        .reshape(entry_count, QUERY_HEADS * HEAD_SIZE)
        .astype(jnp.bfloat16)
    )


def local(
    stream,
    queries,
    fresh_entries,
    paged_store_cache,
    page_table,
    cache_length,
    out_proj,
    norm_gain,
    router,
    routes,
    gate_up,
    down_proj,
):
    tensor_count = lax.axis_size(TENSOR)
    my_index = lax.axis_index(TENSOR)
    dec_rows = queries.shape[0]
    query_all = gather_nested(queries)
    request_max, request_total, request_accum = local_parts(
        query_all, paged_store_cache, page_table, cache_length, my_index
    )
    packed = jnp.concatenate(
        (request_max[..., None], request_total[..., None], request_accum), axis=-1
    )
    packed = packed.reshape((tensor_count, dec_rows) + packed.shape[1:])
    parts = lax.all_to_all(packed, TENSOR, split_axis=0, concat_axis=0, tiled=True)
    parts = jnp.swapaxes(parts, 0, 1)
    context = finish_context(parts, queries, fresh_entries)
    context_all = gather_nested(context)
    projected = jnp.dot(context_all, out_proj, preferred_element_type=jnp.float32)
    column_block = projected.shape[1]
    arrived = lax.all_to_all(
        projected.reshape(tensor_count, dec_rows, column_block),
        TENSOR,
        split_axis=0,
        concat_axis=2,
        tiled=True,
    )
    widened = stream.astype(jnp.float32)
    widened = widened.at[:dec_rows].add(arrived[0])
    resid = lax.optimization_barrier(widened.astype(jnp.bfloat16))
    widened = resid.astype(jnp.float32)
    inverse = lax.rsqrt(jnp.mean(widened * widened, axis=-1, keepdims=True) + EPSILON)
    normed = (widened * inverse * norm_gain.astype(jnp.float32)).astype(jnp.bfloat16)
    logits = jnp.dot(normed, router, preferred_element_type=jnp.float32)
    chosen = jnp.take_along_axis(logits, routes, axis=1)
    gate_probs = jax.nn.softmax(chosen, axis=-1)
    expert_count = tensor_count // GROUP
    expert_ids = jnp.arange(expert_count, dtype=jnp.int32)
    matched = routes[:, :, None] == expert_ids[None, None, :]
    routed = jnp.any(matched, axis=1)
    gate_weight = jnp.sum(jnp.where(matched, gate_probs[:, :, None], 0.0), axis=1)
    routed_count = routed.astype(jnp.int32)
    ranking = jnp.cumsum(routed_count, axis=0) - routed_count
    slot_ids = jnp.arange(CAP, dtype=jnp.int32)
    selector = routed.T[:, None, :] & (ranking.T[:, None, :] == slot_ids[None, :, None])
    slot_rows = jnp.einsum(
        "eci,id->ecd", selector.astype(jnp.bfloat16), normed, preferred_element_type=jnp.float32
    ).astype(jnp.bfloat16)
    contract_last = (((1,), (1,)), ((), ()))
    landed = lax.all_to_all(slot_rows, EXPERT_AXES, split_axis=0, concat_axis=0, tiled=True)
    gathered = lax.all_gather(lax.all_gather(landed, "zl", axis=0), "c", axis=0)
    shape_in = gathered.shape
    flat_rows = gathered.reshape(-1, shape_in[-1])
    gate_part = lax.dot_general(
        flat_rows, gate_up[0], contract_last, preferred_element_type=jnp.float32
    )
    upward = lax.dot_general(
        flat_rows, gate_up[1], contract_last, preferred_element_type=jnp.float32
    )
    active = (jax.nn.silu(gate_part) * upward).astype(jnp.bfloat16)
    partial_value = jnp.dot(active, down_proj, preferred_element_type=jnp.float32).astype(
        jnp.bfloat16
    )
    group_rows = partial_value.astype(jnp.float32).reshape(shape_in)
    core_sum = lax.psum_scatter(group_rows, "c", scatter_dimension=0, tiled=True)
    slice_sum = lax.psum_scatter(
        core_sum.astype(jnp.bfloat16), "zl", scatter_dimension=1, tiled=True
    )
    expert_out = lax.all_to_all(
        slice_sum.reshape(landed.shape), EXPERT_AXES, split_axis=0, concat_axis=0, tiled=True
    ).astype(jnp.float32)
    weighted = selector.astype(jnp.float32) * gate_weight.T[:, None, :]
    routed_sum = jnp.einsum("eci,ecd->id", weighted, expert_out)
    return (widened + routed_sum).astype(jnp.bfloat16)


def physical_mesh(mesh):
    dp_count, tensor_count = mesh.devices.shape
    z_count = tensor_count // 2 // 4
    z_low = GROUP // 2
    shape = (dp_count, 4, z_count // z_low, z_low, 2)
    return Mesh(np.asarray(mesh.devices).reshape(shape), ("dp",) + TENSOR)


def solution(mesh):
    mesh = physical_mesh(mesh)
    rows = ("dp",) + TENSOR
    placed = (
        P(rows, None),
        P(rows, None),
        P(rows, None),
        P(rows, None, None, None),
        P("dp", None),
        P("dp"),
        P(None, TENSOR),
        P(),
        P(),
        P(rows, None),
        P(None, TENSOR, None),
        P(TENSOR, None),
    )
    return jax.shard_map(
        local, mesh=mesh, in_specs=placed, out_specs=P(rows, None), check_vma=False
    )
```

```python
import math

import jax
import jax.numpy as jnp
import numpy as np
from jax import lax
from jax.sharding import Mesh
from jax.sharding import PartitionSpec as P

QUERY_HEADS = 20
KEY_VALUE_HEADS = 4
HEAD_SIZE = 128
GROUP = 8
CAP = 6


NEG_FILL = -1e30
EPSILON = 1e-05

TENSOR = ("y", "zh", "zl", "c")
EXPERT_AXES = ("y", "zh")


def gather_nested(x):
    x = lax.all_gather(x, "c", axis=0, tiled=True)
    x = lax.all_gather(x, ("zh", "zl"), axis=0, tiled=True)
    return lax.all_gather(x, "y", axis=0, tiled=True)


def local_parts(query_all, paged_store_cache, page_table, cache_length, my_index):
    request_page_count = paged_store_cache.shape[0]
    page_length = paged_store_cache.shape[2]
    longest = page_table.shape[1]
    query_groups = QUERY_HEADS // KEY_VALUE_HEADS
    global_ids = my_index * request_page_count + jnp.arange(request_page_count, dtype=jnp.int32)
    matched = page_table[None, :, :] == global_ids[:, None, None]
    owner = jnp.any(matched, axis=2)
    position = jnp.sum(
        jnp.where(matched, jnp.arange(longest, dtype=jnp.int32)[None, None, :], 0), axis=(1, 2)
    )
    length_here = jnp.sum(jnp.where(owner, cache_length[None, :], 0), axis=1)
    query_page_scores = jnp.dot(
        owner.astype(jnp.bfloat16), query_all, preferred_element_type=jnp.float32
    ).astype(jnp.bfloat16)
    query_page_scores = query_page_scores.reshape(
        request_page_count, KEY_VALUE_HEADS, query_groups, HEAD_SIZE
    )
    key_matrix = paged_store_cache[:, 0].reshape(
        request_page_count, page_length, KEY_VALUE_HEADS, HEAD_SIZE
    )
    value_matrix = (
        paged_store_cache[:, 1]
        .reshape(request_page_count, page_length, KEY_VALUE_HEADS, HEAD_SIZE)
        .astype(jnp.float32)
    )
    scores = jnp.einsum(
        "phgd,pthd->phgt", query_page_scores, key_matrix, preferred_element_type=jnp.float32
    ) * (1.0 / math.sqrt(HEAD_SIZE))
    offsets = jnp.arange(page_length, dtype=jnp.int32)
    valid = position[:, None] * page_length + offsets[None, :] < length_here[:, None]
    scores = jnp.where(valid[:, None, None, :], scores, NEG_FILL)
    page_max = jnp.max(scores, axis=-1)
    weights = jnp.exp(scores - page_max[..., None])
    page_total = jnp.sum(weights, axis=-1)
    page_accum = jnp.einsum("phgt,pthd->phgd", weights, value_matrix)
    owned = owner[:, :, None, None]
    request_max = jnp.max(jnp.where(owned, page_max[:, None], NEG_FILL), axis=0)
    coef = jnp.where(owned, jnp.exp(page_max[:, None] - request_max[None]), 0.0)
    request_total = jnp.sum(coef * page_total[:, None], axis=0)
    request_accum = jnp.einsum("prhg,phgd->rhgd", coef, page_accum)
    return (request_max, request_total, request_accum)


def finish_context(parts, local_queries, local_entries):
    entry_count = local_queries.shape[0]
    key_value_width = KEY_VALUE_HEADS * HEAD_SIZE
    query_vector = local_queries.reshape(
        entry_count, KEY_VALUE_HEADS, QUERY_HEADS // KEY_VALUE_HEADS, HEAD_SIZE
    )
    token_key = local_entries[:, :key_value_width].reshape(entry_count, KEY_VALUE_HEADS, HEAD_SIZE)
    token_value = (
        local_entries[:, key_value_width:]
        .reshape(entry_count, KEY_VALUE_HEADS, HEAD_SIZE)
        .astype(jnp.float32)
    )
    own_score = jnp.einsum(
        "rhgd,rhd->rhg", query_vector, token_key, preferred_element_type=jnp.float32
    ) * (1.0 / math.sqrt(HEAD_SIZE))
    part_max = parts[..., 0]
    part_total = parts[..., 1]
    part_accum = parts[..., 2:]
    joined = jnp.maximum(jnp.max(part_max, axis=1), own_score)
    coef = jnp.exp(part_max - joined[:, None])
    own_weight = jnp.exp(own_score - joined)
    totals = jnp.sum(coef * part_total, axis=1) + own_weight
    accum = (
        jnp.sum(coef[..., None] * part_accum, axis=1)
        + own_weight[..., None] * token_value[:, :, None, :]
    )
    return (
        (accum / totals[..., None])
        .reshape(entry_count, QUERY_HEADS * HEAD_SIZE)
        .astype(jnp.bfloat16)
    )


def local(
    stream,
    queries,
    fresh_entries,
    paged_store_cache,
    page_table,
    cache_length,
    out_proj,
    norm_gain,
    router,
    routes,
    gate_up,
    down_proj,
):
    tensor_count = lax.axis_size(TENSOR)
    my_index = lax.axis_index(TENSOR)
    dec_rows = queries.shape[0]
    query_all = gather_nested(queries)
    request_max, request_total, request_accum = local_parts(
        query_all, paged_store_cache, page_table, cache_length, my_index
    )
    packed = jnp.concatenate(
        (request_max[..., None], request_total[..., None], request_accum), axis=-1
    )
    packed = packed.reshape((tensor_count, dec_rows) + packed.shape[1:])
    parts = lax.all_to_all(packed, TENSOR, split_axis=0, concat_axis=0, tiled=True)
    parts = jnp.swapaxes(parts, 0, 1)
    context = finish_context(parts, queries, fresh_entries)
    context_all = gather_nested(context)
    projected = jnp.dot(context_all, out_proj, preferred_element_type=jnp.float32)
    column_block = projected.shape[1]
    arrived = lax.all_to_all(
        projected.reshape(tensor_count, dec_rows, column_block),
        TENSOR,
        split_axis=0,
        concat_axis=2,
        tiled=True,
    )
    widened = stream.astype(jnp.float32)
    widened = widened.at[:dec_rows].add(arrived[0])
    resid = lax.optimization_barrier(widened.astype(jnp.bfloat16))
    widened = resid.astype(jnp.float32)
    inverse = lax.rsqrt(jnp.mean(widened * widened, axis=-1, keepdims=True) + EPSILON)
    normed = (widened * inverse * norm_gain.astype(jnp.float32)).astype(jnp.bfloat16)
    logits = jnp.dot(normed, router, preferred_element_type=jnp.float32)
    chosen = jnp.take_along_axis(logits, routes, axis=1)
    gate_probs = jax.nn.softmax(chosen, axis=-1)
    expert_count = tensor_count // GROUP
    expert_ids = jnp.arange(expert_count, dtype=jnp.int32)
    matched = routes[:, :, None] == expert_ids[None, None, :]
    routed = jnp.any(matched, axis=1)
    gate_weight = jnp.sum(jnp.where(matched, gate_probs[:, :, None], 0.0), axis=1)
    routed_count = routed.astype(jnp.int32)
    ranking = jnp.cumsum(routed_count, axis=0) - routed_count
    slot_ids = jnp.arange(CAP, dtype=jnp.int32)
    selector = routed.T[None, :, :] & (ranking.T[None, :, :] == slot_ids[:, None, None])
    slot_rows = jnp.einsum(
        "cei,id->ced", selector.astype(jnp.bfloat16), normed, preferred_element_type=jnp.float32
    ).astype(jnp.bfloat16)
    landed = lax.all_to_all(slot_rows, EXPERT_AXES, split_axis=1, concat_axis=1, tiled=True)
    own_rows = lax.all_gather(landed, "zl", axis=0)
    swap = [(0, 1), (1, 0)]
    partner_rows = lax.ppermute(own_rows, "c", swap)

    def expert_partial(rows):
        flat_rows = rows.reshape(-1, rows.shape[-1])
        contract_last = (((1,), (1,)), ((), ()))
        gate_part = lax.dot_general(
            flat_rows, gate_up[0], contract_last, preferred_element_type=jnp.float32
        )
        upward = lax.dot_general(
            flat_rows, gate_up[1], contract_last, preferred_element_type=jnp.float32
        )
        active = (jax.nn.silu(gate_part) * upward).astype(jnp.bfloat16)
        partial_value = jnp.dot(active, down_proj, preferred_element_type=jnp.float32)
        return partial_value.astype(jnp.bfloat16).astype(jnp.float32).reshape(rows.shape)

    own_partial = expert_partial(own_rows)
    partner_partial = expert_partial(partner_rows)
    core_sum = own_partial + lax.ppermute(partner_partial, "c", swap)
    slice_sum = lax.psum_scatter(
        core_sum.astype(jnp.bfloat16), "zl", scatter_dimension=0, tiled=True
    )
    expert_out = lax.all_to_all(
        slice_sum.reshape(landed.shape), EXPERT_AXES, split_axis=1, concat_axis=1, tiled=True
    ).astype(jnp.float32)
    weighted = selector.astype(jnp.float32) * gate_weight.T[None, :, :]
    routed_sum = jnp.einsum("cei,ced->id", weighted, expert_out)
    return (widened + routed_sum).astype(jnp.bfloat16)


def physical_mesh(mesh):
    dp_count, tensor_count = mesh.devices.shape
    z_count = tensor_count // 2 // 4
    z_low = GROUP // 2
    shape = (dp_count, 4, z_count // z_low, z_low, 2)
    return Mesh(np.asarray(mesh.devices).reshape(shape), ("dp",) + TENSOR)


def solution(mesh):
    mesh = physical_mesh(mesh)
    rows = ("dp",) + TENSOR
    placed = (
        P(rows, None),
        P(rows, None),
        P(rows, None),
        P(rows, None, None, None),
        P("dp", None),
        P("dp"),
        P(None, TENSOR),
        P(),
        P(),
        P(rows, None),
        P(None, TENSOR, None),
        P(TENSOR, None),
    )
    return jax.shard_map(
        local, mesh=mesh, in_specs=placed, out_specs=P(rows, None), check_vma=False
    )
```

```python
import math

import jax
import jax.numpy as jnp
import numpy as np
from jax import lax
from jax.sharding import Mesh
from jax.sharding import PartitionSpec as P

QUERY_HEADS = 20
KEY_VALUE_HEADS = 4
HEAD_SIZE = 128
GROUP = 8
CAP = 6


NEG_FILL = -1e30
EPSILON = 1e-05

TENSOR = ("y", "zh", "zl", "c")
EXPERT_AXES = ("y", "zh")


def gather_nested(x):
    x = lax.all_gather(x, "c", axis=0, tiled=True)
    x = lax.all_gather(x, ("zh", "zl"), axis=0, tiled=True)
    return lax.all_gather(x, "y", axis=0, tiled=True)


def local_parts(query_all, paged_store_cache, page_table, cache_length, my_index):
    request_page_count = paged_store_cache.shape[0]
    page_length = paged_store_cache.shape[2]
    longest = page_table.shape[1]
    query_groups = QUERY_HEADS // KEY_VALUE_HEADS
    global_ids = my_index * request_page_count + jnp.arange(request_page_count, dtype=jnp.int32)
    matched = page_table[None, :, :] == global_ids[:, None, None]
    owner = jnp.any(matched, axis=2)
    position = jnp.sum(
        jnp.where(matched, jnp.arange(longest, dtype=jnp.int32)[None, None, :], 0), axis=(1, 2)
    )
    length_here = jnp.sum(jnp.where(owner, cache_length[None, :], 0), axis=1)
    query_page_scores = jnp.dot(
        owner.astype(jnp.bfloat16), query_all, preferred_element_type=jnp.float32
    ).astype(jnp.bfloat16)
    query_page_scores = query_page_scores.reshape(
        request_page_count, KEY_VALUE_HEADS, query_groups, HEAD_SIZE
    )
    key_matrix = paged_store_cache[:, 0].reshape(
        request_page_count, page_length, KEY_VALUE_HEADS, HEAD_SIZE
    )
    value_matrix = (
        paged_store_cache[:, 1]
        .reshape(request_page_count, page_length, KEY_VALUE_HEADS, HEAD_SIZE)
        .astype(jnp.float32)
    )
    scores = jnp.einsum(
        "phgd,pthd->phgt", query_page_scores, key_matrix, preferred_element_type=jnp.float32
    ) * (1.0 / math.sqrt(HEAD_SIZE))
    offsets = jnp.arange(page_length, dtype=jnp.int32)
    valid = position[:, None] * page_length + offsets[None, :] < length_here[:, None]
    scores = jnp.where(valid[:, None, None, :], scores, NEG_FILL)
    page_max = jnp.max(scores, axis=-1)
    weights = jnp.exp(scores - page_max[..., None])
    page_total = jnp.sum(weights, axis=-1)
    page_accum = jnp.einsum("phgt,pthd->phgd", weights, value_matrix)
    owned = owner[:, :, None, None]
    request_max = jnp.max(jnp.where(owned, page_max[:, None], NEG_FILL), axis=0)
    coef = jnp.where(owned, jnp.exp(page_max[:, None] - request_max[None]), 0.0)
    request_total = jnp.sum(coef * page_total[:, None], axis=0)
    request_accum = jnp.einsum("prhg,phgd->rhgd", coef, page_accum)
    return (request_max, request_total, request_accum)


def finish_context(parts, local_queries, local_entries):
    entry_count = local_queries.shape[0]
    key_value_width = KEY_VALUE_HEADS * HEAD_SIZE
    query_vector = local_queries.reshape(
        entry_count, KEY_VALUE_HEADS, QUERY_HEADS // KEY_VALUE_HEADS, HEAD_SIZE
    )
    token_key = local_entries[:, :key_value_width].reshape(entry_count, KEY_VALUE_HEADS, HEAD_SIZE)
    token_value = (
        local_entries[:, key_value_width:]
        .reshape(entry_count, KEY_VALUE_HEADS, HEAD_SIZE)
        .astype(jnp.float32)
    )
    own_score = jnp.einsum(
        "rhgd,rhd->rhg", query_vector, token_key, preferred_element_type=jnp.float32
    ) * (1.0 / math.sqrt(HEAD_SIZE))
    parts = parts.astype(jnp.float32)
    part_max = parts[..., 0] + parts[..., 1]
    part_total = parts[..., 2]
    part_accum = parts[..., 3:]
    joined = jnp.maximum(jnp.max(part_max, axis=1), own_score)
    coef = jnp.exp(part_max - joined[:, None])
    own_weight = jnp.exp(own_score - joined)
    totals = jnp.sum(coef * part_total, axis=1) + own_weight
    accum = (
        jnp.sum(coef[..., None] * part_accum, axis=1)
        + own_weight[..., None] * token_value[:, :, None, :]
    )
    return (
        (accum / totals[..., None])
        .reshape(entry_count, QUERY_HEADS * HEAD_SIZE)
        .astype(jnp.bfloat16)
    )


def local(
    stream,
    queries,
    fresh_entries,
    paged_store_cache,
    page_table,
    cache_length,
    out_proj,
    norm_gain,
    router,
    routes,
    gate_up,
    down_proj,
):
    tensor_count = lax.axis_size(TENSOR)
    my_index = lax.axis_index(TENSOR)
    dec_rows = queries.shape[0]
    query_all = gather_nested(queries)
    request_max, request_total, request_accum = local_parts(
        query_all, paged_store_cache, page_table, cache_length, my_index
    )
    max_high = lax.reduce_precision(request_max, exponent_bits=8, mantissa_bits=7)
    max_low = lax.reduce_precision(request_max - max_high, exponent_bits=8, mantissa_bits=7)
    rebase = jnp.where(
        request_max > 0.5 * NEG_FILL, jnp.exp(request_max - (max_high + max_low)), 0.0
    )
    packed = jnp.concatenate(
        (
            max_high[..., None],
            max_low[..., None],
            (request_total * rebase)[..., None],
            request_accum * rebase[..., None],
        ),
        axis=-1,
    ).astype(jnp.bfloat16)
    packed = packed.reshape((tensor_count, dec_rows) + packed.shape[1:])
    parts = lax.all_to_all(packed, TENSOR, split_axis=0, concat_axis=0, tiled=True)
    parts = jnp.swapaxes(parts, 0, 1)
    context = finish_context(parts, queries, fresh_entries)
    context_all = gather_nested(context)
    projected = jnp.dot(context_all, out_proj, preferred_element_type=jnp.float32)
    column_block = projected.shape[1]
    arrived = lax.all_to_all(
        projected.reshape(tensor_count, dec_rows, column_block),
        TENSOR,
        split_axis=0,
        concat_axis=2,
        tiled=True,
    )
    widened = stream.astype(jnp.float32)
    widened = widened.at[:dec_rows].add(arrived[0])
    resid = lax.optimization_barrier(widened.astype(jnp.bfloat16))
    widened = resid.astype(jnp.float32)
    inverse = lax.rsqrt(jnp.mean(widened * widened, axis=-1, keepdims=True) + EPSILON)
    normed = (widened * inverse * norm_gain.astype(jnp.float32)).astype(jnp.bfloat16)
    logits = jnp.dot(normed, router, preferred_element_type=jnp.float32)
    chosen = jnp.take_along_axis(logits, routes, axis=1)
    gate_probs = jax.nn.softmax(chosen, axis=-1)
    expert_count = tensor_count // GROUP
    expert_ids = jnp.arange(expert_count, dtype=jnp.int32)
    matched = routes[:, :, None] == expert_ids[None, None, :]
    routed = jnp.any(matched, axis=1)
    gate_weight = jnp.sum(jnp.where(matched, gate_probs[:, :, None], 0.0), axis=1)
    routed_count = routed.astype(jnp.int32)
    ranking = jnp.cumsum(routed_count, axis=0) - routed_count
    slot_ids = jnp.arange(CAP, dtype=jnp.int32)
    selector = routed.T[None, :, :] & (ranking.T[None, :, :] == slot_ids[:, None, None])
    slot_rows = jnp.einsum(
        "cei,id->ced", selector.astype(jnp.bfloat16), normed, preferred_element_type=jnp.float32
    ).astype(jnp.bfloat16)
    landed = lax.all_to_all(slot_rows, EXPERT_AXES, split_axis=1, concat_axis=1, tiled=True)
    own_rows = lax.all_gather(landed, "zl", axis=0)
    swap = [(0, 1), (1, 0)]
    partner_rows = lax.ppermute(own_rows, "c", swap)

    def expert_partial(rows):
        flat_rows = rows.reshape(-1, rows.shape[-1])
        contract_last = (((1,), (1,)), ((), ()))
        gate_part = lax.dot_general(
            flat_rows, gate_up[0], contract_last, preferred_element_type=jnp.float32
        )
        upward = lax.dot_general(
            flat_rows, gate_up[1], contract_last, preferred_element_type=jnp.float32
        )
        active = (jax.nn.silu(gate_part) * upward).astype(jnp.bfloat16)
        partial_value = jnp.dot(active, down_proj, preferred_element_type=jnp.float32)
        return partial_value.astype(jnp.bfloat16).astype(jnp.float32).reshape(rows.shape)

    own_partial = expert_partial(own_rows)
    partner_partial = expert_partial(partner_rows)
    core_sum = own_partial + lax.ppermute(partner_partial, "c", swap)
    slice_sum = lax.psum_scatter(
        core_sum.astype(jnp.bfloat16), "zl", scatter_dimension=0, tiled=True
    )
    expert_out = lax.all_to_all(
        slice_sum.reshape(landed.shape), EXPERT_AXES, split_axis=1, concat_axis=1, tiled=True
    ).astype(jnp.float32)
    weighted = selector.astype(jnp.float32) * gate_weight.T[None, :, :]
    routed_sum = jnp.einsum("cei,ced->id", weighted, expert_out)
    return (widened + routed_sum).astype(jnp.bfloat16)


def physical_mesh(mesh):
    dp_count, tensor_count = mesh.devices.shape
    z_count = tensor_count // 2 // 4
    z_low = GROUP // 2
    shape = (dp_count, 4, z_count // z_low, z_low, 2)
    return Mesh(np.asarray(mesh.devices).reshape(shape), ("dp",) + TENSOR)


def solution(mesh):
    mesh = physical_mesh(mesh)
    rows = ("dp",) + TENSOR
    placed = (
        P(rows, None),
        P(rows, None),
        P(rows, None),
        P(rows, None, None, None),
        P("dp", None),
        P("dp"),
        P(None, TENSOR),
        P(),
        P(),
        P(rows, None),
        P(None, TENSOR, None),
        P(TENSOR, None),
    )
    return jax.shard_map(
        local, mesh=mesh, in_specs=placed, out_specs=P(rows, None), check_vma=False
    )
```

```python
import math

import jax
import jax.numpy as jnp
import numpy as np
from jax import lax
from jax.sharding import Mesh
from jax.sharding import PartitionSpec as P

QUERY_HEADS = 20
KEY_VALUE_HEADS = 4
HEAD_SIZE = 128
GROUP = 8
CAP = 6


NEG_FILL = -1e30
EPSILON = 1e-05

TENSOR = ("y", "zh", "zl", "c")
EXPERT_AXES = ("y", "zh")


def gather_axis(x, axis, count):
    me = lax.axis_index(axis)
    pieces = [x] + [
        lax.ppermute(x, axis, [(i, (i + k) % count) for i in range(count)]) for k in range(1, count)
    ]
    order = (me - jnp.arange(count, dtype=jnp.int32)) % count
    gathered = jnp.take(jnp.stack(pieces), order, axis=0)
    return gathered.reshape((count * x.shape[0],) + x.shape[1:])


def scatter_sum_axis(x, axis, count):
    me = lax.axis_index(axis)
    total = jnp.take(x, me, axis=0).astype(jnp.float32)
    for k in range(1, count):
        block = jnp.take(x, (me + k) % count, axis=0)
        total = total + lax.ppermute(block, axis, [(i, (i + k) % count) for i in range(count)]).astype(jnp.float32)
    return total


def gather_nested(x, sizes):
    for axis in reversed(TENSOR):
        x = gather_axis(x, axis, sizes[axis])
    return x


def local_parts(query_all, paged_store_cache, page_table, cache_length, my_index):
    request_page_count = paged_store_cache.shape[0]
    page_length = paged_store_cache.shape[2]
    longest = page_table.shape[1]
    query_groups = QUERY_HEADS // KEY_VALUE_HEADS
    global_ids = my_index * request_page_count + jnp.arange(request_page_count, dtype=jnp.int32)
    matched = page_table[None, :, :] == global_ids[:, None, None]
    owner = jnp.any(matched, axis=2)
    position = jnp.sum(
        jnp.where(matched, jnp.arange(longest, dtype=jnp.int32)[None, None, :], 0), axis=(1, 2)
    )
    length_here = jnp.sum(jnp.where(owner, cache_length[None, :], 0), axis=1)
    query_page_scores = jnp.dot(
        owner.astype(jnp.bfloat16), query_all, preferred_element_type=jnp.float32
    ).astype(jnp.bfloat16)
    query_page_scores = query_page_scores.reshape(
        request_page_count, KEY_VALUE_HEADS, query_groups, HEAD_SIZE
    )
    key_matrix = paged_store_cache[:, 0].reshape(
        request_page_count, page_length, KEY_VALUE_HEADS, HEAD_SIZE
    )
    value_matrix = (
        paged_store_cache[:, 1]
        .reshape(request_page_count, page_length, KEY_VALUE_HEADS, HEAD_SIZE)
        .astype(jnp.float32)
    )
    scores = jnp.einsum(
        "phgd,pthd->phgt", query_page_scores, key_matrix, preferred_element_type=jnp.float32
    ) * (1.0 / math.sqrt(HEAD_SIZE))
    offsets = jnp.arange(page_length, dtype=jnp.int32)
    valid = position[:, None] * page_length + offsets[None, :] < length_here[:, None]
    scores = jnp.where(valid[:, None, None, :], scores, NEG_FILL)
    page_max = jnp.max(scores, axis=-1)
    weights = jnp.exp(scores - page_max[..., None])
    page_total = jnp.sum(weights, axis=-1)
    page_accum = jnp.einsum("phgt,pthd->phgd", weights, value_matrix)
    owned = owner[:, :, None, None]
    request_max = jnp.max(jnp.where(owned, page_max[:, None], NEG_FILL), axis=0)
    coef = jnp.where(owned, jnp.exp(page_max[:, None] - request_max[None]), 0.0)
    request_total = jnp.sum(coef * page_total[:, None], axis=0)
    request_accum = jnp.einsum("prhg,phgd->rhgd", coef, page_accum)
    return (request_max, request_total, request_accum)


def finish_context(parts, local_queries, local_entries):
    entry_count = local_queries.shape[0]
    key_value_width = KEY_VALUE_HEADS * HEAD_SIZE
    query_vector = local_queries.reshape(
        entry_count, KEY_VALUE_HEADS, QUERY_HEADS // KEY_VALUE_HEADS, HEAD_SIZE
    )
    token_key = local_entries[:, :key_value_width].reshape(entry_count, KEY_VALUE_HEADS, HEAD_SIZE)
    token_value = (
        local_entries[:, key_value_width:]
        .reshape(entry_count, KEY_VALUE_HEADS, HEAD_SIZE)
        .astype(jnp.float32)
    )
    own_score = jnp.einsum(
        "rhgd,rhd->rhg", query_vector, token_key, preferred_element_type=jnp.float32
    ) * (1.0 / math.sqrt(HEAD_SIZE))
    parts = parts.astype(jnp.float32)
    part_max = parts[..., 0] + parts[..., 1]
    part_total = parts[..., 2]
    part_accum = parts[..., 3:]
    joined = jnp.maximum(jnp.max(part_max, axis=1), own_score)
    coef = jnp.exp(part_max - joined[:, None])
    own_weight = jnp.exp(own_score - joined)
    totals = jnp.sum(coef * part_total, axis=1) + own_weight
    accum = (
        jnp.sum(coef[..., None] * part_accum, axis=1)
        + own_weight[..., None] * token_value[:, :, None, :]
    )
    return (
        (accum / totals[..., None])
        .reshape(entry_count, QUERY_HEADS * HEAD_SIZE)
        .astype(jnp.bfloat16)
    )


def local(
    stream,
    queries,
    fresh_entries,
    paged_store_cache,
    page_table,
    cache_length,
    out_proj,
    norm_gain,
    router,
    routes,
    gate_up,
    down_proj,
):
    tensor_count = lax.axis_size(TENSOR)
    my_index = lax.axis_index(TENSOR)
    dec_rows = queries.shape[0]
    sizes = {axis: lax.axis_size(axis) for axis in TENSOR}
    query_all = gather_nested(queries, sizes)
    request_max, request_total, request_accum = local_parts(
        query_all, paged_store_cache, page_table, cache_length, my_index
    )
    max_high = lax.reduce_precision(request_max, exponent_bits=8, mantissa_bits=7)
    max_low = lax.reduce_precision(request_max - max_high, exponent_bits=8, mantissa_bits=7)
    rebase = jnp.where(
        request_max > 0.5 * NEG_FILL, jnp.exp(request_max - (max_high + max_low)), 0.0
    )
    packed = jnp.concatenate(
        (
            max_high[..., None],
            max_low[..., None],
            (request_total * rebase)[..., None],
            request_accum * rebase[..., None],
        ),
        axis=-1,
    ).astype(jnp.bfloat16)
    packed = packed.reshape((tensor_count, dec_rows) + packed.shape[1:])
    parts = lax.all_to_all(packed, TENSOR, split_axis=0, concat_axis=0, tiled=True)
    parts = jnp.swapaxes(parts, 0, 1)
    context = finish_context(parts, queries, fresh_entries)
    context_all = gather_nested(context, sizes)
    projected = jnp.dot(context_all, out_proj, preferred_element_type=jnp.float32)
    column_block = projected.shape[1]
    arrived = lax.all_to_all(
        projected.reshape(tensor_count, dec_rows, column_block),
        TENSOR,
        split_axis=0,
        concat_axis=2,
        tiled=True,
    )
    widened = stream.astype(jnp.float32)
    widened = widened.at[:dec_rows].add(arrived[0])
    resid = lax.optimization_barrier(widened.astype(jnp.bfloat16))
    widened = resid.astype(jnp.float32)
    inverse = lax.rsqrt(jnp.mean(widened * widened, axis=-1, keepdims=True) + EPSILON)
    normed = (widened * inverse * norm_gain.astype(jnp.float32)).astype(jnp.bfloat16)
    logits = jnp.dot(normed, router, preferred_element_type=jnp.float32)
    chosen = jnp.take_along_axis(logits, routes, axis=1)
    gate_probs = jax.nn.softmax(chosen, axis=-1)
    expert_count = tensor_count // GROUP
    expert_ids = jnp.arange(expert_count, dtype=jnp.int32)
    matched = routes[:, :, None] == expert_ids[None, None, :]
    routed = jnp.any(matched, axis=1)
    gate_weight = jnp.sum(jnp.where(matched, gate_probs[:, :, None], 0.0), axis=1)
    routed_count = routed.astype(jnp.int32)
    ranking = jnp.cumsum(routed_count, axis=0) - routed_count
    slot_ids = jnp.arange(CAP, dtype=jnp.int32)
    selector = routed.T[None, :, :] & (ranking.T[None, :, :] == slot_ids[:, None, None])
    slot_rows = jnp.einsum(
        "cei,id->ced", selector.astype(jnp.bfloat16), normed, preferred_element_type=jnp.float32
    ).astype(jnp.bfloat16)
    landed = lax.all_to_all(slot_rows, EXPERT_AXES, split_axis=1, concat_axis=1, tiled=True)
    own_rows = gather_axis(landed[None], "zl", sizes["zl"])
    swap = [(0, 1), (1, 0)]
    partner_rows = lax.ppermute(own_rows, "c", swap)

    def expert_partial(rows):
        flat_rows = rows.reshape(-1, rows.shape[-1])
        contract_last = (((1,), (1,)), ((), ()))
        gate_part = lax.dot_general(
            flat_rows, gate_up[0], contract_last, preferred_element_type=jnp.float32
        )
        upward = lax.dot_general(
            flat_rows, gate_up[1], contract_last, preferred_element_type=jnp.float32
        )
        active = (jax.nn.silu(gate_part) * upward).astype(jnp.bfloat16)
        partial_value = jnp.dot(active, down_proj, preferred_element_type=jnp.float32)
        return partial_value.astype(jnp.bfloat16).astype(jnp.float32).reshape(rows.shape)

    own_partial = expert_partial(own_rows)
    partner_partial = expert_partial(partner_rows)
    core_sum = own_partial + lax.ppermute(partner_partial, "c", swap)
    slice_sum = scatter_sum_axis(core_sum.astype(jnp.bfloat16), "zl", sizes["zl"])
    expert_out = lax.all_to_all(
        slice_sum.astype(jnp.bfloat16), EXPERT_AXES, split_axis=1, concat_axis=1, tiled=True
    ).astype(jnp.float32)
    weighted = selector.astype(jnp.float32) * gate_weight.T[None, :, :]
    routed_sum = jnp.einsum("cei,ced->id", weighted, expert_out)
    return (widened + routed_sum).astype(jnp.bfloat16)


def physical_mesh(mesh):
    dp_count, tensor_count = mesh.devices.shape
    z_count = tensor_count // 2 // 4
    z_low = GROUP // 2
    shape = (dp_count, 4, z_count // z_low, z_low, 2)
    return Mesh(np.asarray(mesh.devices).reshape(shape), ("dp",) + TENSOR)


def solution(mesh):
    mesh = physical_mesh(mesh)
    rows = ("dp",) + TENSOR
    placed = (
        P(rows, None),
        P(rows, None),
        P(rows, None),
        P(rows, None, None, None),
        P("dp", None),
        P("dp"),
        P(None, TENSOR),
        P(),
        P(),
        P(rows, None),
        P(None, TENSOR, None),
        P(TENSOR, None),
    )
    return jax.shard_map(
        local, mesh=mesh, in_specs=placed, out_specs=P(rows, None), check_vma=False
    )
```

```python
import math

import jax
import jax.numpy as jnp
import numpy as np
from jax import lax
from jax.sharding import Mesh
from jax.sharding import PartitionSpec as P

QUERY_HEADS = 20
KEY_VALUE_HEADS = 4
HEAD_SIZE = 128
GROUP = 8
CAP = 6


NEG_FILL = -1e30
EPSILON = 1e-05

TENSOR = ("y", "zh", "zl", "c")
EXPERT_AXES = ("y", "zh")


def gather_axis(x, axis, count):
    me = lax.axis_index(axis)
    pieces = [x] + [
        lax.ppermute(x, axis, [(i, (i + k) % count) for i in range(count)]) for k in range(1, count)
    ]
    order = (me - jnp.arange(count, dtype=jnp.int32)) % count
    gathered = jnp.take(jnp.stack(pieces), order, axis=0)
    return gathered.reshape((count * x.shape[0],) + x.shape[1:])


def scatter_sum_axis(x, axis, count):
    me = lax.axis_index(axis)
    total = jnp.take(x, me, axis=0).astype(jnp.float32)
    for k in range(1, count):
        block = jnp.take(x, (me + k) % count, axis=0)
        total = total + lax.ppermute(block, axis, [(i, (i + k) % count) for i in range(count)]).astype(jnp.float32)
    return total


def gather_nested(x):
    x = lax.all_gather(x, "c", axis=0, tiled=True)
    x = lax.all_gather(x, ("zh", "zl"), axis=0, tiled=True)
    return lax.all_gather(x, "y", axis=0, tiled=True)


def local_parts(query_all, paged_store_cache, page_table, cache_length, my_index):
    request_page_count = paged_store_cache.shape[0]
    page_length = paged_store_cache.shape[2]
    longest = page_table.shape[1]
    query_groups = QUERY_HEADS // KEY_VALUE_HEADS
    global_ids = my_index * request_page_count + jnp.arange(request_page_count, dtype=jnp.int32)
    matched = page_table[None, :, :] == global_ids[:, None, None]
    owner = jnp.any(matched, axis=2)
    position = jnp.sum(
        jnp.where(matched, jnp.arange(longest, dtype=jnp.int32)[None, None, :], 0), axis=(1, 2)
    )
    length_here = jnp.sum(jnp.where(owner, cache_length[None, :], 0), axis=1)
    query_page_scores = jnp.dot(
        owner.astype(jnp.bfloat16), query_all, preferred_element_type=jnp.float32
    ).astype(jnp.bfloat16)
    query_page_scores = query_page_scores.reshape(
        request_page_count, KEY_VALUE_HEADS, query_groups, HEAD_SIZE
    )
    key_matrix = paged_store_cache[:, 0].reshape(
        request_page_count, page_length, KEY_VALUE_HEADS, HEAD_SIZE
    )
    value_matrix = (
        paged_store_cache[:, 1]
        .reshape(request_page_count, page_length, KEY_VALUE_HEADS, HEAD_SIZE)
        .astype(jnp.float32)
    )
    scores = jnp.einsum(
        "phgd,pthd->phgt", query_page_scores, key_matrix, preferred_element_type=jnp.float32
    ) * (1.0 / math.sqrt(HEAD_SIZE))
    offsets = jnp.arange(page_length, dtype=jnp.int32)
    valid = position[:, None] * page_length + offsets[None, :] < length_here[:, None]
    scores = jnp.where(valid[:, None, None, :], scores, NEG_FILL)
    page_max = jnp.max(scores, axis=-1)
    weights = jnp.exp(scores - page_max[..., None])
    page_total = jnp.sum(weights, axis=-1)
    page_accum = jnp.einsum("phgt,pthd->phgd", weights, value_matrix)
    owned = owner[:, :, None, None]
    request_max = jnp.max(jnp.where(owned, page_max[:, None], NEG_FILL), axis=0)
    coef = jnp.where(owned, jnp.exp(page_max[:, None] - request_max[None]), 0.0)
    request_total = jnp.sum(coef * page_total[:, None], axis=0)
    request_accum = jnp.einsum("prhg,phgd->rhgd", coef, page_accum)
    return (request_max, request_total, request_accum)


def finish_context(parts, local_queries, local_entries):
    entry_count = local_queries.shape[0]
    key_value_width = KEY_VALUE_HEADS * HEAD_SIZE
    query_vector = local_queries.reshape(
        entry_count, KEY_VALUE_HEADS, QUERY_HEADS // KEY_VALUE_HEADS, HEAD_SIZE
    )
    token_key = local_entries[:, :key_value_width].reshape(entry_count, KEY_VALUE_HEADS, HEAD_SIZE)
    token_value = (
        local_entries[:, key_value_width:]
        .reshape(entry_count, KEY_VALUE_HEADS, HEAD_SIZE)
        .astype(jnp.float32)
    )
    own_score = jnp.einsum(
        "rhgd,rhd->rhg", query_vector, token_key, preferred_element_type=jnp.float32
    ) * (1.0 / math.sqrt(HEAD_SIZE))
    parts = parts.astype(jnp.float32)
    part_max = parts[..., 0] + parts[..., 1]
    part_total = parts[..., 2]
    part_accum = parts[..., 3:]
    joined = jnp.maximum(jnp.max(part_max, axis=1), own_score)
    coef = jnp.exp(part_max - joined[:, None])
    own_weight = jnp.exp(own_score - joined)
    totals = jnp.sum(coef * part_total, axis=1) + own_weight
    accum = (
        jnp.sum(coef[..., None] * part_accum, axis=1)
        + own_weight[..., None] * token_value[:, :, None, :]
    )
    return (
        (accum / totals[..., None])
        .reshape(entry_count, QUERY_HEADS * HEAD_SIZE)
        .astype(jnp.bfloat16)
    )


def local(
    stream,
    queries,
    fresh_entries,
    paged_store_cache,
    page_table,
    cache_length,
    out_proj,
    norm_gain,
    router,
    routes,
    gate_up,
    down_proj,
):
    tensor_count = lax.axis_size(TENSOR)
    my_index = lax.axis_index(TENSOR)
    dec_rows = queries.shape[0]
    sizes = {axis: lax.axis_size(axis) for axis in TENSOR}
    query_all = gather_nested(queries)
    request_max, request_total, request_accum = local_parts(
        query_all, paged_store_cache, page_table, cache_length, my_index
    )
    max_high = lax.reduce_precision(request_max, exponent_bits=8, mantissa_bits=7)
    max_low = lax.reduce_precision(request_max - max_high, exponent_bits=8, mantissa_bits=7)
    rebase = jnp.where(
        request_max > 0.5 * NEG_FILL, jnp.exp(request_max - (max_high + max_low)), 0.0
    )
    packed = jnp.concatenate(
        (
            max_high[..., None],
            max_low[..., None],
            (request_total * rebase)[..., None],
            request_accum * rebase[..., None],
        ),
        axis=-1,
    ).astype(jnp.bfloat16)
    packed = packed.reshape((tensor_count, dec_rows) + packed.shape[1:])
    parts = lax.all_to_all(packed, TENSOR, split_axis=0, concat_axis=0, tiled=True)
    parts = jnp.swapaxes(parts, 0, 1)
    context = finish_context(parts, queries, fresh_entries)
    context_all = gather_nested(context)
    projected = jnp.dot(context_all, out_proj, preferred_element_type=jnp.float32)
    column_block = projected.shape[1]
    arrived = lax.all_to_all(
        projected.reshape(tensor_count, dec_rows, column_block),
        TENSOR,
        split_axis=0,
        concat_axis=2,
        tiled=True,
    )
    widened = stream.astype(jnp.float32)
    prefill = widened[dec_rows:]
    prefill_sum = routed_experts(
        rms_norm(prefill, norm_gain), routes[dec_rows:], router, gate_up, down_proj, CAP, sizes
    )
    decode = lax.reduce_precision(widened[:dec_rows] + arrived[0], exponent_bits=8, mantissa_bits=7)
    decode_sum = routed_experts(
        rms_norm(decode, norm_gain), routes[:dec_rows], router, gate_up, down_proj, dec_rows, sizes
    )
    return jnp.concatenate((decode + decode_sum, prefill + prefill_sum)).astype(jnp.bfloat16)


def rms_norm(widened, norm_gain):
    inverse = lax.rsqrt(jnp.mean(widened * widened, axis=-1, keepdims=True) + EPSILON)
    return (widened * inverse * norm_gain.astype(jnp.float32)).astype(jnp.bfloat16)


def routed_experts(normed, routes, router, gate_up, down_proj, capacity, sizes):
    tensor_count = lax.axis_size(TENSOR)
    logits = jnp.dot(normed, router, preferred_element_type=jnp.float32)
    chosen = jnp.take_along_axis(logits, routes, axis=1)
    gate_probs = jax.nn.softmax(chosen, axis=-1)
    expert_count = tensor_count // GROUP
    expert_ids = jnp.arange(expert_count, dtype=jnp.int32)
    matched = routes[:, :, None] == expert_ids[None, None, :]
    routed = jnp.any(matched, axis=1)
    gate_weight = jnp.sum(jnp.where(matched, gate_probs[:, :, None], 0.0), axis=1)
    routed_count = routed.astype(jnp.int32)
    ranking = jnp.cumsum(routed_count, axis=0) - routed_count
    slot_ids = jnp.arange(capacity, dtype=jnp.int32)
    selector = routed.T[None, :, :] & (ranking.T[None, :, :] == slot_ids[:, None, None])
    slot_rows = jnp.einsum(
        "cei,id->ced", selector.astype(jnp.bfloat16), normed, preferred_element_type=jnp.float32
    ).astype(jnp.bfloat16)
    landed = lax.all_to_all(slot_rows, EXPERT_AXES, split_axis=1, concat_axis=1, tiled=True)
    own_rows = gather_axis(landed[None], "zl", sizes["zl"])
    swap = [(0, 1), (1, 0)]
    partner_rows = lax.ppermute(own_rows, "c", swap)

    def expert_partial(rows):
        flat_rows = rows.reshape(-1, rows.shape[-1])
        contract_last = (((1,), (1,)), ((), ()))
        gate_part = lax.dot_general(
            flat_rows, gate_up[0], contract_last, preferred_element_type=jnp.float32
        )
        upward = lax.dot_general(
            flat_rows, gate_up[1], contract_last, preferred_element_type=jnp.float32
        )
        active = (jax.nn.silu(gate_part) * upward).astype(jnp.bfloat16)
        partial_value = jnp.dot(active, down_proj, preferred_element_type=jnp.float32)
        return partial_value.astype(jnp.bfloat16).astype(jnp.float32).reshape(rows.shape)

    own_partial = expert_partial(own_rows)
    partner_partial = expert_partial(partner_rows)
    core_sum = own_partial + lax.ppermute(partner_partial, "c", swap)
    slice_sum = scatter_sum_axis(core_sum.astype(jnp.bfloat16), "zl", sizes["zl"])
    expert_out = lax.all_to_all(
        slice_sum.astype(jnp.bfloat16), EXPERT_AXES, split_axis=1, concat_axis=1, tiled=True
    ).astype(jnp.float32)
    weighted = selector.astype(jnp.float32) * gate_weight.T[None, :, :]
    routed_sum = jnp.einsum("cei,ced->id", weighted, expert_out)
    return routed_sum


def physical_mesh(mesh):
    dp_count, tensor_count = mesh.devices.shape
    z_count = tensor_count // 2 // 4
    z_low = GROUP // 2
    shape = (dp_count, 4, z_count // z_low, z_low, 2)
    return Mesh(np.asarray(mesh.devices).reshape(shape), ("dp",) + TENSOR)


def solution(mesh):
    mesh = physical_mesh(mesh)
    rows = ("dp",) + TENSOR
    placed = (
        P(rows, None),
        P(rows, None),
        P(rows, None),
        P(rows, None, None, None),
        P("dp", None),
        P("dp"),
        P(None, TENSOR),
        P(),
        P(),
        P(rows, None),
        P(None, TENSOR, None),
        P(TENSOR, None),
    )
    return jax.shard_map(
        local, mesh=mesh, in_specs=placed, out_specs=P(rows, None), check_vma=False
    )
```

```python
import math

import jax
import jax.numpy as jnp
import numpy as np
from jax import lax
from jax.sharding import Mesh
from jax.sharding import PartitionSpec as P

QUERY_HEADS = 20
KEY_VALUE_HEADS = 4
HEAD_SIZE = 128
GROUP = 8
CAP = 6


NEG_FILL = -1e30
EPSILON = 1e-05

TENSOR = ("y", "zh", "zl", "c")
EXPERT_AXES = ("y", "zh")


def gather_axis(x, axis, count):
    me = lax.axis_index(axis)
    pieces = [x] + [
        lax.ppermute(x, axis, [(i, (i + k) % count) for i in range(count)]) for k in range(1, count)
    ]
    order = (me - jnp.arange(count, dtype=jnp.int32)) % count
    gathered = jnp.take(jnp.stack(pieces), order, axis=0)
    return gathered.reshape((count * x.shape[0],) + x.shape[1:])


def scatter_sum_axis(x, axis, count):
    me = lax.axis_index(axis)
    total = jnp.take(x, me, axis=0).astype(jnp.float32)
    for k in range(1, count):
        block = jnp.take(x, (me + k) % count, axis=0)
        total = total + lax.ppermute(block, axis, [(i, (i + k) % count) for i in range(count)]).astype(jnp.float32)
    return total


def gather_nested(x):
    x = lax.all_gather(x, "c", axis=0, tiled=True)
    x = lax.all_gather(x, ("zh", "zl"), axis=0, tiled=True)
    return lax.all_gather(x, "y", axis=0, tiled=True)


def local_parts(query_all, paged_store_cache, page_table, cache_length, my_index):
    request_page_count = paged_store_cache.shape[0]
    page_length = paged_store_cache.shape[2]
    longest = page_table.shape[1]
    query_groups = QUERY_HEADS // KEY_VALUE_HEADS
    global_ids = my_index * request_page_count + jnp.arange(request_page_count, dtype=jnp.int32)
    matched = page_table[None, :, :] == global_ids[:, None, None]
    owner = jnp.any(matched, axis=2)
    position = jnp.sum(
        jnp.where(matched, jnp.arange(longest, dtype=jnp.int32)[None, None, :], 0), axis=(1, 2)
    )
    length_here = jnp.sum(jnp.where(owner, cache_length[None, :], 0), axis=1)
    query_page_scores = jnp.dot(
        owner.astype(jnp.bfloat16), query_all, preferred_element_type=jnp.float32
    ).astype(jnp.bfloat16)
    query_page_scores = query_page_scores.reshape(
        request_page_count, KEY_VALUE_HEADS, query_groups, HEAD_SIZE
    )
    key_matrix = paged_store_cache[:, 0].reshape(
        request_page_count, page_length, KEY_VALUE_HEADS, HEAD_SIZE
    )
    value_matrix = (
        paged_store_cache[:, 1]
        .reshape(request_page_count, page_length, KEY_VALUE_HEADS, HEAD_SIZE)
        .astype(jnp.float32)
    )
    scores = jnp.einsum(
        "phgd,pthd->phgt", query_page_scores, key_matrix, preferred_element_type=jnp.float32
    ) * (1.0 / math.sqrt(HEAD_SIZE))
    offsets = jnp.arange(page_length, dtype=jnp.int32)
    valid = position[:, None] * page_length + offsets[None, :] < length_here[:, None]
    scores = jnp.where(valid[:, None, None, :], scores, NEG_FILL)
    page_max = jnp.max(scores, axis=-1)
    weights = jnp.exp(scores - page_max[..., None])
    page_total = jnp.sum(weights, axis=-1)
    page_accum = jnp.einsum("phgt,pthd->phgd", weights, value_matrix)
    owned = owner[:, :, None, None]
    request_max = jnp.max(jnp.where(owned, page_max[:, None], NEG_FILL), axis=0)
    coef = jnp.where(owned, jnp.exp(page_max[:, None] - request_max[None]), 0.0)
    request_total = jnp.sum(coef * page_total[:, None], axis=0)
    request_accum = jnp.einsum("prhg,phgd->rhgd", coef, page_accum)
    return (request_max, request_total, request_accum)


def finish_context(parts, local_queries, local_entries):
    entry_count = local_queries.shape[0]
    key_value_width = KEY_VALUE_HEADS * HEAD_SIZE
    query_vector = local_queries.reshape(
        entry_count, KEY_VALUE_HEADS, QUERY_HEADS // KEY_VALUE_HEADS, HEAD_SIZE
    )
    token_key = local_entries[:, :key_value_width].reshape(entry_count, KEY_VALUE_HEADS, HEAD_SIZE)
    token_value = (
        local_entries[:, key_value_width:]
        .reshape(entry_count, KEY_VALUE_HEADS, HEAD_SIZE)
        .astype(jnp.float32)
    )
    own_score = jnp.einsum(
        "rhgd,rhd->rhg", query_vector, token_key, preferred_element_type=jnp.float32
    ) * (1.0 / math.sqrt(HEAD_SIZE))
    parts = parts.astype(jnp.float32)
    part_max = parts[..., 0] + parts[..., 1]
    part_total = parts[..., 2]
    part_accum = parts[..., 3:]
    joined = jnp.maximum(jnp.max(part_max, axis=1), own_score)
    coef = jnp.exp(part_max - joined[:, None])
    own_weight = jnp.exp(own_score - joined)
    totals = jnp.sum(coef * part_total, axis=1) + own_weight
    accum = (
        jnp.sum(coef[..., None] * part_accum, axis=1)
        + own_weight[..., None] * token_value[:, :, None, :]
    )
    return (
        (accum / totals[..., None])
        .reshape(entry_count, QUERY_HEADS * HEAD_SIZE)
        .astype(jnp.bfloat16)
    )


def local(
    stream,
    queries,
    fresh_entries,
    paged_store_cache,
    page_table,
    cache_length,
    out_proj,
    norm_gain,
    router,
    routes,
    gate_up,
    down_proj,
):
    tensor_count = lax.axis_size(TENSOR)
    my_index = lax.axis_index(TENSOR)
    dec_rows = queries.shape[0]
    query_all = gather_nested(queries)
    request_max, request_total, request_accum = local_parts(
        query_all, paged_store_cache, page_table, cache_length, my_index
    )
    max_high = lax.reduce_precision(request_max, exponent_bits=8, mantissa_bits=7)
    max_low = lax.reduce_precision(request_max - max_high, exponent_bits=8, mantissa_bits=7)
    rebase = jnp.where(
        request_max > 0.5 * NEG_FILL, jnp.exp(request_max - (max_high + max_low)), 0.0
    )
    packed = jnp.concatenate(
        (
            max_high[..., None],
            max_low[..., None],
            (request_total * rebase)[..., None],
            request_accum * rebase[..., None],
        ),
        axis=-1,
    ).astype(jnp.bfloat16)
    packed = packed.reshape((tensor_count, dec_rows) + packed.shape[1:])
    parts = lax.all_to_all(packed, TENSOR, split_axis=0, concat_axis=0, tiled=True)
    parts = jnp.swapaxes(parts, 0, 1)
    context = finish_context(parts, queries, fresh_entries)
    context_all = gather_nested(context)
    projected = jnp.dot(context_all, out_proj, preferred_element_type=jnp.float32)
    column_block = projected.shape[1]
    arrived = lax.all_to_all(
        projected.reshape(tensor_count, dec_rows, column_block),
        TENSOR,
        split_axis=0,
        concat_axis=2,
        tiled=True,
    )
    widened = stream.astype(jnp.float32)
    widened = widened.at[:dec_rows].add(arrived[0])
    resid = lax.optimization_barrier(widened.astype(jnp.bfloat16))
    widened = resid.astype(jnp.float32)
    inverse = lax.rsqrt(jnp.mean(widened * widened, axis=-1, keepdims=True) + EPSILON)
    normed = (widened * inverse * norm_gain.astype(jnp.float32)).astype(jnp.bfloat16)
    logits = jnp.dot(normed, router, preferred_element_type=jnp.float32)
    chosen = jnp.take_along_axis(logits, routes, axis=1)
    gate_probs = jax.nn.softmax(chosen, axis=-1)
    expert_count = tensor_count // GROUP
    expert_ids = jnp.arange(expert_count, dtype=jnp.int32)
    matched = routes[:, :, None] == expert_ids[None, None, :]
    routed = jnp.any(matched, axis=1)
    gate_weight = jnp.sum(jnp.where(matched, gate_probs[:, :, None], 0.0), axis=1)
    routed_count = routed.astype(jnp.int32)
    ranking = jnp.cumsum(routed_count, axis=0) - routed_count
    slot_ids = jnp.arange(CAP, dtype=jnp.int32)
    selector = routed.T[None, :, :] & (ranking.T[None, :, :] == slot_ids[:, None, None])
    slot_rows = jnp.einsum(
        "cei,id->ced", selector.astype(jnp.bfloat16), normed, preferred_element_type=jnp.float32
    ).astype(jnp.bfloat16)
    landed = lax.all_to_all(slot_rows, EXPERT_AXES, split_axis=1, concat_axis=1, tiled=True)
    z_low = lax.axis_size("zl")
    own_rows = gather_axis(landed[None], "zl", z_low)
    swap = [(0, 1), (1, 0)]
    partner_rows = lax.ppermute(own_rows, "c", swap)

    def expert_partial(rows):
        flat_rows = rows.reshape(-1, rows.shape[-1])
        contract_last = (((1,), (1,)), ((), ()))
        gate_part = lax.dot_general(
            flat_rows, gate_up[0], contract_last, preferred_element_type=jnp.float32
        )
        upward = lax.dot_general(
            flat_rows, gate_up[1], contract_last, preferred_element_type=jnp.float32
        )
        active = (jax.nn.silu(gate_part) * upward).astype(jnp.bfloat16)
        partial_value = jnp.dot(active, down_proj, preferred_element_type=jnp.float32)
        return partial_value.astype(jnp.bfloat16).astype(jnp.float32).reshape(rows.shape)

    own_partial = expert_partial(own_rows)
    partner_partial = expert_partial(partner_rows)
    core_sum = own_partial + lax.ppermute(partner_partial, "c", swap)
    slice_sum = scatter_sum_axis(core_sum.astype(jnp.bfloat16), "zl", z_low)
    expert_out = lax.all_to_all(
        slice_sum.astype(jnp.bfloat16), EXPERT_AXES, split_axis=1, concat_axis=1, tiled=True
    ).astype(jnp.float32)
    weighted = selector.astype(jnp.float32) * gate_weight.T[None, :, :]
    routed_sum = jnp.einsum("cei,ced->id", weighted, expert_out)
    return (widened + routed_sum).astype(jnp.bfloat16)


def physical_mesh(mesh):
    dp_count, tensor_count = mesh.devices.shape
    z_count = tensor_count // 2 // 4
    z_low = GROUP // 2
    shape = (dp_count, 4, z_count // z_low, z_low, 2)
    return Mesh(np.asarray(mesh.devices).reshape(shape), ("dp",) + TENSOR)


def solution(mesh):
    mesh = physical_mesh(mesh)
    rows = ("dp",) + TENSOR
    placed = (
        P(rows, None),
        P(rows, None),
        P(rows, None),
        P(rows, None, None, None),
        P("dp", None),
        P("dp"),
        P(None, TENSOR),
        P(),
        P(),
        P(rows, None),
        P(None, TENSOR, None),
        P(TENSOR, None),
    )
    return jax.shard_map(
        local, mesh=mesh, in_specs=placed, out_specs=P(rows, None), check_vma=False
    )
```

```python
import math

import jax
import jax.numpy as jnp
import numpy as np
from jax import lax
from jax.sharding import Mesh
from jax.sharding import PartitionSpec as P

QUERY_HEADS = 20
KEY_VALUE_HEADS = 4
HEAD_SIZE = 128
GROUP = 8
CAP = 6


NEG_FILL = -1e30
EPSILON = 1e-05

TENSOR = ("y", "zh", "zl", "c")
EXPERT_AXES = ("y", "zh")


def gather_axis(x, axis, count):
    me = lax.axis_index(axis)
    pieces = [x] + [
        lax.ppermute(x, axis, [(i, (i + k) % count) for i in range(count)]) for k in range(1, count)
    ]
    order = (me - jnp.arange(count, dtype=jnp.int32)) % count
    gathered = jnp.take(jnp.stack(pieces), order, axis=0)
    return gathered.reshape((count * x.shape[0],) + x.shape[1:])


def scatter_sum_axis(x, axis, count):
    me = lax.axis_index(axis)
    total = jnp.take(x, me, axis=0).astype(jnp.float32)
    for k in range(1, count):
        block = jnp.take(x, (me + k) % count, axis=0)
        total = total + lax.ppermute(block, axis, [(i, (i + k) % count) for i in range(count)]).astype(jnp.float32)
    return total


def gather_nested(x):
    x = lax.all_gather(x, "c", axis=0, tiled=True)
    x = lax.all_gather(x, "zl", axis=0, tiled=True)
    x = lax.all_gather(x, "zh", axis=0, tiled=True)
    return lax.all_gather(x, "y", axis=0, tiled=True)


def local_parts(query_all, paged_store_cache, page_table, cache_length, my_index):
    request_page_count = paged_store_cache.shape[0]
    page_length = paged_store_cache.shape[2]
    longest = page_table.shape[1]
    query_groups = QUERY_HEADS // KEY_VALUE_HEADS
    global_ids = my_index * request_page_count + jnp.arange(request_page_count, dtype=jnp.int32)
    matched = page_table[None, :, :] == global_ids[:, None, None]
    owner = jnp.any(matched, axis=2)
    position = jnp.sum(
        jnp.where(matched, jnp.arange(longest, dtype=jnp.int32)[None, None, :], 0), axis=(1, 2)
    )
    length_here = jnp.sum(jnp.where(owner, cache_length[None, :], 0), axis=1)
    query_page_scores = jnp.dot(
        owner.astype(jnp.bfloat16), query_all, preferred_element_type=jnp.float32
    ).astype(jnp.bfloat16)
    query_page_scores = query_page_scores.reshape(
        request_page_count, KEY_VALUE_HEADS, query_groups, HEAD_SIZE
    )
    key_matrix = paged_store_cache[:, 0].reshape(
        request_page_count, page_length, KEY_VALUE_HEADS, HEAD_SIZE
    )
    value_matrix = (
        paged_store_cache[:, 1]
        .reshape(request_page_count, page_length, KEY_VALUE_HEADS, HEAD_SIZE)
        .astype(jnp.float32)
    )
    scores = jnp.einsum(
        "phgd,pthd->phgt", query_page_scores, key_matrix, preferred_element_type=jnp.float32
    ) * (1.0 / math.sqrt(HEAD_SIZE))
    offsets = jnp.arange(page_length, dtype=jnp.int32)
    valid = position[:, None] * page_length + offsets[None, :] < length_here[:, None]
    scores = jnp.where(valid[:, None, None, :], scores, NEG_FILL)
    page_max = jnp.max(scores, axis=-1)
    weights = jnp.exp(scores - page_max[..., None])
    page_total = jnp.sum(weights, axis=-1)
    page_accum = jnp.einsum("phgt,pthd->phgd", weights, value_matrix)
    owned = owner[:, :, None, None]
    request_max = jnp.max(jnp.where(owned, page_max[:, None], NEG_FILL), axis=0)
    coef = jnp.where(owned, jnp.exp(page_max[:, None] - request_max[None]), 0.0)
    request_total = jnp.sum(coef * page_total[:, None], axis=0)
    request_accum = jnp.einsum("prhg,phgd->rhgd", coef, page_accum)
    return (request_max, request_total, request_accum)


def finish_context(parts, local_queries, local_entries):
    entry_count = local_queries.shape[0]
    key_value_width = KEY_VALUE_HEADS * HEAD_SIZE
    query_vector = local_queries.reshape(
        entry_count, KEY_VALUE_HEADS, QUERY_HEADS // KEY_VALUE_HEADS, HEAD_SIZE
    )
    token_key = local_entries[:, :key_value_width].reshape(entry_count, KEY_VALUE_HEADS, HEAD_SIZE)
    token_value = (
        local_entries[:, key_value_width:]
        .reshape(entry_count, KEY_VALUE_HEADS, HEAD_SIZE)
        .astype(jnp.float32)
    )
    own_score = jnp.einsum(
        "rhgd,rhd->rhg", query_vector, token_key, preferred_element_type=jnp.float32
    ) * (1.0 / math.sqrt(HEAD_SIZE))
    parts = parts.astype(jnp.float32)
    part_max = parts[..., 0] + parts[..., 1]
    part_total = parts[..., 2]
    part_accum = parts[..., 3:]
    joined = jnp.maximum(jnp.max(part_max, axis=1), own_score)
    coef = jnp.exp(part_max - joined[:, None])
    own_weight = jnp.exp(own_score - joined)
    totals = jnp.sum(coef * part_total, axis=1) + own_weight
    accum = (
        jnp.sum(coef[..., None] * part_accum, axis=1)
        + own_weight[..., None] * token_value[:, :, None, :]
    )
    return (
        (accum / totals[..., None])
        .reshape(entry_count, QUERY_HEADS * HEAD_SIZE)
        .astype(jnp.bfloat16)
    )


def local(
    stream,
    queries,
    fresh_entries,
    paged_store_cache,
    page_table,
    cache_length,
    out_proj,
    norm_gain,
    router,
    routes,
    gate_up,
    down_proj,
):
    tensor_count = lax.axis_size(TENSOR)
    my_index = lax.axis_index(TENSOR)
    dec_rows = queries.shape[0]
    query_all = gather_nested(queries)
    request_max, request_total, request_accum = local_parts(
        query_all, paged_store_cache, page_table, cache_length, my_index
    )
    max_high = lax.reduce_precision(request_max, exponent_bits=8, mantissa_bits=7)
    max_low = lax.reduce_precision(request_max - max_high, exponent_bits=8, mantissa_bits=7)
    rebase = jnp.where(
        request_max > 0.5 * NEG_FILL, jnp.exp(request_max - (max_high + max_low)), 0.0
    )
    packed = jnp.concatenate(
        (
            max_high[..., None],
            max_low[..., None],
            (request_total * rebase)[..., None],
            request_accum * rebase[..., None],
        ),
        axis=-1,
    ).astype(jnp.bfloat16)
    packed = packed.reshape((tensor_count, dec_rows) + packed.shape[1:])
    parts = lax.all_to_all(packed, TENSOR, split_axis=0, concat_axis=0, tiled=True)
    parts = jnp.swapaxes(parts, 0, 1)
    context = finish_context(parts, queries, fresh_entries)
    context_all = gather_nested(context)
    projected = jnp.dot(context_all, out_proj, preferred_element_type=jnp.float32)
    column_block = projected.shape[1]
    arrived = lax.all_to_all(
        projected.reshape(tensor_count, dec_rows, column_block),
        TENSOR,
        split_axis=0,
        concat_axis=2,
        tiled=True,
    )
    widened = stream.astype(jnp.float32)
    widened = widened.at[:dec_rows].add(arrived[0])
    resid = lax.optimization_barrier(widened.astype(jnp.bfloat16))
    widened = resid.astype(jnp.float32)
    inverse = lax.rsqrt(jnp.mean(widened * widened, axis=-1, keepdims=True) + EPSILON)
    normed = (widened * inverse * norm_gain.astype(jnp.float32)).astype(jnp.bfloat16)
    logits = jnp.dot(normed, router, preferred_element_type=jnp.float32)
    chosen = jnp.take_along_axis(logits, routes, axis=1)
    gate_probs = jax.nn.softmax(chosen, axis=-1)
    expert_count = tensor_count // GROUP
    expert_ids = jnp.arange(expert_count, dtype=jnp.int32)
    matched = routes[:, :, None] == expert_ids[None, None, :]
    routed = jnp.any(matched, axis=1)
    gate_weight = jnp.sum(jnp.where(matched, gate_probs[:, :, None], 0.0), axis=1)
    routed_count = routed.astype(jnp.int32)
    ranking = jnp.cumsum(routed_count, axis=0) - routed_count
    slot_ids = jnp.arange(CAP, dtype=jnp.int32)
    selector = routed.T[None, :, :] & (ranking.T[None, :, :] == slot_ids[:, None, None])
    slot_rows = jnp.einsum(
        "cei,id->ced", selector.astype(jnp.bfloat16), normed, preferred_element_type=jnp.float32
    ).astype(jnp.bfloat16)
    landed = lax.all_to_all(slot_rows, EXPERT_AXES, split_axis=1, concat_axis=1, tiled=True)
    z_low = lax.axis_size("zl")
    own_rows = gather_axis(landed[None], "zl", z_low)
    swap = [(0, 1), (1, 0)]
    partner_rows = lax.ppermute(own_rows, "c", swap)

    def expert_partial(rows):
        flat_rows = rows.reshape(-1, rows.shape[-1])
        contract_last = (((1,), (1,)), ((), ()))
        gate_part = lax.dot_general(
            flat_rows, gate_up[0], contract_last, preferred_element_type=jnp.float32
        )
        upward = lax.dot_general(
            flat_rows, gate_up[1], contract_last, preferred_element_type=jnp.float32
        )
        active = (jax.nn.silu(gate_part) * upward).astype(jnp.bfloat16)
        partial_value = jnp.dot(active, down_proj, preferred_element_type=jnp.float32)
        return partial_value.astype(jnp.bfloat16).astype(jnp.float32).reshape(rows.shape)

    own_partial = expert_partial(own_rows)
    partner_partial = expert_partial(partner_rows)
    core_sum = own_partial + lax.ppermute(partner_partial, "c", swap)
    slice_sum = scatter_sum_axis(core_sum.astype(jnp.bfloat16), "zl", z_low)
    expert_out = lax.all_to_all(
        slice_sum.astype(jnp.bfloat16), EXPERT_AXES, split_axis=1, concat_axis=1, tiled=True
    ).astype(jnp.float32)
    weighted = selector.astype(jnp.float32) * gate_weight.T[None, :, :]
    routed_sum = jnp.einsum("cei,ced->id", weighted, expert_out)
    return (widened + routed_sum).astype(jnp.bfloat16)


def physical_mesh(mesh):
    dp_count, tensor_count = mesh.devices.shape
    z_count = tensor_count // 2 // 4
    z_low = GROUP // 2
    shape = (dp_count, 4, z_count // z_low, z_low, 2)
    return Mesh(np.asarray(mesh.devices).reshape(shape), ("dp",) + TENSOR)


def solution(mesh):
    mesh = physical_mesh(mesh)
    rows = ("dp",) + TENSOR
    placed = (
        P(rows, None),
        P(rows, None),
        P(rows, None),
        P(rows, None, None, None),
        P("dp", None),
        P("dp"),
        P(None, TENSOR),
        P(),
        P(),
        P(rows, None),
        P(None, TENSOR, None),
        P(TENSOR, None),
    )
    return jax.shard_map(
        local, mesh=mesh, in_specs=placed, out_specs=P(rows, None), check_vma=False
    )
```

```python
import math

import jax
import jax.numpy as jnp
import numpy as np
from jax import lax
from jax.sharding import Mesh
from jax.sharding import PartitionSpec as P

QUERY_HEADS = 20
KEY_VALUE_HEADS = 4
HEAD_SIZE = 128
GROUP = 8
CAP = 6


NEG_FILL = -1e30
EPSILON = 1e-05

TENSOR = ("y", "zh", "zl", "c")
EXPERT_AXES = ("y", "zh")


def gather_axis(x, axis, count):
    me = lax.axis_index(axis)
    pieces = [x] + [
        lax.ppermute(x, axis, [(i, (i + k) % count) for i in range(count)]) for k in range(1, count)
    ]
    order = (me - jnp.arange(count, dtype=jnp.int32)) % count
    gathered = jnp.take(jnp.stack(pieces), order, axis=0)
    return gathered.reshape((count * x.shape[0],) + x.shape[1:])


def scatter_sum_axis(x, axis, count):
    me = lax.axis_index(axis)
    total = jnp.take(x, me, axis=0).astype(jnp.float32)
    for k in range(1, count):
        block = jnp.take(x, (me + k) % count, axis=0)
        total = total + lax.ppermute(block, axis, [(i, (i + k) % count) for i in range(count)]).astype(jnp.float32)
    return total


def gather_nested(x):
    x = lax.all_gather(x, "c", axis=0, tiled=True)
    x = lax.all_gather(x, ("zh", "zl"), axis=0, tiled=True)
    return lax.all_gather(x, "y", axis=0, tiled=True)


def local_parts(query_all, paged_store_cache, page_table, cache_length, my_index):
    request_page_count = paged_store_cache.shape[0]
    page_length = paged_store_cache.shape[2]
    longest = page_table.shape[1]
    query_groups = QUERY_HEADS // KEY_VALUE_HEADS
    global_ids = my_index * request_page_count + jnp.arange(request_page_count, dtype=jnp.int32)
    matched = page_table[None, :, :] == global_ids[:, None, None]
    owner = jnp.any(matched, axis=2)
    position = jnp.sum(
        jnp.where(matched, jnp.arange(longest, dtype=jnp.int32)[None, None, :], 0), axis=(1, 2)
    )
    length_here = jnp.sum(jnp.where(owner, cache_length[None, :], 0), axis=1)
    query_page_scores = jnp.dot(
        owner.astype(jnp.bfloat16), query_all, preferred_element_type=jnp.float32
    ).astype(jnp.bfloat16)
    query_page_scores = query_page_scores.reshape(
        request_page_count, KEY_VALUE_HEADS, query_groups, HEAD_SIZE
    )
    key_matrix = paged_store_cache[:, 0].reshape(
        request_page_count, page_length, KEY_VALUE_HEADS, HEAD_SIZE
    )
    value_matrix = (
        paged_store_cache[:, 1]
        .reshape(request_page_count, page_length, KEY_VALUE_HEADS, HEAD_SIZE)
        .astype(jnp.float32)
    )
    scores = jnp.einsum(
        "phgd,pthd->phgt", query_page_scores, key_matrix, preferred_element_type=jnp.float32
    ) * (1.0 / math.sqrt(HEAD_SIZE))
    offsets = jnp.arange(page_length, dtype=jnp.int32)
    valid = position[:, None] * page_length + offsets[None, :] < length_here[:, None]
    scores = jnp.where(valid[:, None, None, :], scores, NEG_FILL)
    page_max = jnp.max(scores, axis=-1)
    weights = jnp.exp(scores - page_max[..., None])
    page_total = jnp.sum(weights, axis=-1)
    page_accum = jnp.einsum("phgt,pthd->phgd", weights, value_matrix)
    owned = owner[:, :, None, None]
    request_max = jnp.max(jnp.where(owned, page_max[:, None], NEG_FILL), axis=0)
    coef = jnp.where(owned, jnp.exp(page_max[:, None] - request_max[None]), 0.0)
    request_total = jnp.sum(coef * page_total[:, None], axis=0)
    request_accum = jnp.einsum("prhg,phgd->rhgd", coef, page_accum)
    return (request_max, request_total, request_accum)


def finish_context(parts, local_queries, local_entries):
    entry_count = local_queries.shape[0]
    key_value_width = KEY_VALUE_HEADS * HEAD_SIZE
    query_vector = local_queries.reshape(
        entry_count, KEY_VALUE_HEADS, QUERY_HEADS // KEY_VALUE_HEADS, HEAD_SIZE
    )
    token_key = local_entries[:, :key_value_width].reshape(entry_count, KEY_VALUE_HEADS, HEAD_SIZE)
    token_value = (
        local_entries[:, key_value_width:]
        .reshape(entry_count, KEY_VALUE_HEADS, HEAD_SIZE)
        .astype(jnp.float32)
    )
    own_score = jnp.einsum(
        "rhgd,rhd->rhg", query_vector, token_key, preferred_element_type=jnp.float32
    ) * (1.0 / math.sqrt(HEAD_SIZE))
    parts = parts.astype(jnp.float32)
    part_max = parts[..., 0] + parts[..., 1]
    part_total = parts[..., 2]
    part_accum = parts[..., 3:]
    joined = jnp.maximum(jnp.max(part_max, axis=1), own_score)
    coef = jnp.exp(part_max - joined[:, None])
    own_weight = jnp.exp(own_score - joined)
    totals = jnp.sum(coef * part_total, axis=1) + own_weight
    accum = (
        jnp.sum(coef[..., None] * part_accum, axis=1)
        + own_weight[..., None] * token_value[:, :, None, :]
    )
    return (
        (accum / totals[..., None])
        .reshape(entry_count, QUERY_HEADS * HEAD_SIZE)
        .astype(jnp.bfloat16)
    )


def local(
    stream,
    queries,
    fresh_entries,
    paged_store_cache,
    page_table,
    cache_length,
    out_proj,
    norm_gain,
    router,
    routes,
    gate_up,
    down_proj,
):
    tensor_count = lax.axis_size(TENSOR)
    my_index = lax.axis_index(TENSOR)
    dec_rows = queries.shape[0]
    query_all = gather_nested(queries)
    request_max, request_total, request_accum = local_parts(
        query_all, paged_store_cache, page_table, cache_length, my_index
    )
    max_high = lax.reduce_precision(request_max, exponent_bits=8, mantissa_bits=7)
    max_low = lax.reduce_precision(request_max - max_high, exponent_bits=8, mantissa_bits=7)
    rebase = jnp.where(
        request_max > 0.5 * NEG_FILL, jnp.exp(request_max - (max_high + max_low)), 0.0
    )
    packed = jnp.concatenate(
        (
            max_high[..., None],
            max_low[..., None],
            (request_total * rebase)[..., None],
            request_accum * rebase[..., None],
        ),
        axis=-1,
    ).astype(jnp.bfloat16)
    part_shape = packed.shape[1:]
    packed = packed.reshape(tensor_count, dec_rows, -1)
    parts = lax.all_to_all(packed, TENSOR, split_axis=0, concat_axis=0, tiled=True)
    parts = jnp.swapaxes(parts.reshape((tensor_count, dec_rows) + part_shape), 0, 1)
    context = finish_context(parts, queries, fresh_entries)
    context_all = gather_nested(context)
    projected = jnp.dot(context_all, out_proj, preferred_element_type=jnp.float32)
    column_block = projected.shape[1]
    arrived = lax.all_to_all(
        projected.reshape(tensor_count, dec_rows, column_block),
        TENSOR,
        split_axis=0,
        concat_axis=2,
        tiled=True,
    )
    widened = stream.astype(jnp.float32)
    widened = widened.at[:dec_rows].add(arrived[0])
    resid = lax.optimization_barrier(widened.astype(jnp.bfloat16))
    widened = resid.astype(jnp.float32)
    inverse = lax.rsqrt(jnp.mean(widened * widened, axis=-1, keepdims=True) + EPSILON)
    normed = (widened * inverse * norm_gain.astype(jnp.float32)).astype(jnp.bfloat16)
    logits = jnp.dot(normed, router, preferred_element_type=jnp.float32)
    chosen = jnp.take_along_axis(logits, routes, axis=1)
    gate_probs = jax.nn.softmax(chosen, axis=-1)
    expert_count = tensor_count // GROUP
    expert_ids = jnp.arange(expert_count, dtype=jnp.int32)
    matched = routes[:, :, None] == expert_ids[None, None, :]
    routed = jnp.any(matched, axis=1)
    gate_weight = jnp.sum(jnp.where(matched, gate_probs[:, :, None], 0.0), axis=1)
    routed_count = routed.astype(jnp.int32)
    ranking = jnp.cumsum(routed_count, axis=0) - routed_count
    slot_ids = jnp.arange(CAP, dtype=jnp.int32)
    selector = routed.T[None, :, :] & (ranking.T[None, :, :] == slot_ids[:, None, None])
    slot_rows = jnp.einsum(
        "cei,id->ced", selector.astype(jnp.bfloat16), normed, preferred_element_type=jnp.float32
    ).astype(jnp.bfloat16)
    landed = lax.all_to_all(slot_rows, EXPERT_AXES, split_axis=1, concat_axis=1, tiled=True)
    z_low = lax.axis_size("zl")
    own_rows = gather_axis(landed[None], "zl", z_low)
    swap = [(0, 1), (1, 0)]
    partner_rows = lax.ppermute(own_rows, "c", swap)

    def expert_partial(rows):
        flat_rows = rows.reshape(-1, rows.shape[-1])
        contract_last = (((1,), (1,)), ((), ()))
        gate_part = lax.dot_general(
            flat_rows, gate_up[0], contract_last, preferred_element_type=jnp.float32
        )
        upward = lax.dot_general(
            flat_rows, gate_up[1], contract_last, preferred_element_type=jnp.float32
        )
        active = (jax.nn.silu(gate_part) * upward).astype(jnp.bfloat16)
        partial_value = jnp.dot(active, down_proj, preferred_element_type=jnp.float32)
        return partial_value.astype(jnp.bfloat16).astype(jnp.float32).reshape(rows.shape)

    own_partial = expert_partial(own_rows)
    partner_partial = expert_partial(partner_rows)
    core_sum = own_partial + lax.ppermute(partner_partial, "c", swap)
    slice_sum = scatter_sum_axis(core_sum.astype(jnp.bfloat16), "zl", z_low)
    expert_out = lax.all_to_all(
        slice_sum.astype(jnp.bfloat16), EXPERT_AXES, split_axis=1, concat_axis=1, tiled=True
    ).astype(jnp.float32)
    weighted = selector.astype(jnp.float32) * gate_weight.T[None, :, :]
    routed_sum = jnp.einsum("cei,ced->id", weighted, expert_out)
    return (widened + routed_sum).astype(jnp.bfloat16)


def physical_mesh(mesh):
    dp_count, tensor_count = mesh.devices.shape
    z_count = tensor_count // 2 // 4
    z_low = GROUP // 2
    shape = (dp_count, 4, z_count // z_low, z_low, 2)
    return Mesh(np.asarray(mesh.devices).reshape(shape), ("dp",) + TENSOR)


def solution(mesh):
    mesh = physical_mesh(mesh)
    rows = ("dp",) + TENSOR
    placed = (
        P(rows, None),
        P(rows, None),
        P(rows, None),
        P(rows, None, None, None),
        P("dp", None),
        P("dp"),
        P(None, TENSOR),
        P(),
        P(),
        P(rows, None),
        P(None, TENSOR, None),
        P(TENSOR, None),
    )
    return jax.shard_map(
        local, mesh=mesh, in_specs=placed, out_specs=P(rows, None), check_vma=False
    )
```

```python
import math

import jax
import jax.numpy as jnp
import numpy as np
from jax import lax
from jax.sharding import Mesh
from jax.sharding import PartitionSpec as P

QUERY_HEADS = 20
KEY_VALUE_HEADS = 4
HEAD_SIZE = 128
GROUP = 8
CAP = 6


NEG_FILL = -1e30
EPSILON = 1e-05

TENSOR = ("y", "zh", "zl", "c")
EXPERT_AXES = ("y", "zh")


def gather_axis(x, axis, count):
    me = lax.axis_index(axis)
    pieces = [x] + [
        lax.ppermute(x, axis, [(i, (i + k) % count) for i in range(count)]) for k in range(1, count)
    ]
    order = (me - jnp.arange(count, dtype=jnp.int32)) % count
    gathered = jnp.take(jnp.stack(pieces), order, axis=0)
    return gathered.reshape((count * x.shape[0],) + x.shape[1:])


def scatter_sum_axis(x, axis, count):
    me = lax.axis_index(axis)
    total = jnp.take(x, me, axis=0).astype(jnp.float32)
    for k in range(1, count):
        block = jnp.take(x, (me + k) % count, axis=0)
        total = total + lax.ppermute(block, axis, [(i, (i + k) % count) for i in range(count)]).astype(jnp.float32)
    return total


def gather_nested(x):
    x = lax.all_gather(x, "c", axis=0, tiled=True)
    x = lax.all_gather(x, ("zh", "zl"), axis=0, tiled=True)
    return lax.all_gather(x, "y", axis=0, tiled=True)


def local_parts(query_all, paged_store_cache, page_table, cache_length, my_index):
    request_page_count = paged_store_cache.shape[0]
    page_length = paged_store_cache.shape[2]
    longest = page_table.shape[1]
    query_groups = QUERY_HEADS // KEY_VALUE_HEADS
    global_ids = my_index * request_page_count + jnp.arange(request_page_count, dtype=jnp.int32)
    matched = page_table[None, :, :] == global_ids[:, None, None]
    owner = jnp.any(matched, axis=2)
    position = jnp.sum(
        jnp.where(matched, jnp.arange(longest, dtype=jnp.int32)[None, None, :], 0), axis=(1, 2)
    )
    length_here = jnp.sum(jnp.where(owner, cache_length[None, :], 0), axis=1)
    query_page_scores = jnp.dot(
        owner.astype(jnp.bfloat16), query_all, preferred_element_type=jnp.float32
    ).astype(jnp.bfloat16)
    query_page_scores = query_page_scores.reshape(
        request_page_count, KEY_VALUE_HEADS, query_groups, HEAD_SIZE
    )
    key_matrix = paged_store_cache[:, 0].reshape(
        request_page_count, page_length, KEY_VALUE_HEADS, HEAD_SIZE
    )
    value_matrix = (
        paged_store_cache[:, 1]
        .reshape(request_page_count, page_length, KEY_VALUE_HEADS, HEAD_SIZE)
        .astype(jnp.float32)
    )
    scores = jnp.einsum(
        "phgd,pthd->phgt", query_page_scores, key_matrix, preferred_element_type=jnp.float32
    ) * (1.0 / math.sqrt(HEAD_SIZE))
    offsets = jnp.arange(page_length, dtype=jnp.int32)
    valid = position[:, None] * page_length + offsets[None, :] < length_here[:, None]
    scores = jnp.where(valid[:, None, None, :], scores, NEG_FILL)
    page_max = jnp.max(scores, axis=-1)
    weights = jnp.exp(scores - page_max[..., None])
    page_total = jnp.sum(weights, axis=-1)
    page_accum = jnp.einsum("phgt,pthd->phgd", weights, value_matrix)
    owned = owner[:, :, None, None]
    request_max = jnp.max(jnp.where(owned, page_max[:, None], NEG_FILL), axis=0)
    coef = jnp.where(owned, jnp.exp(page_max[:, None] - request_max[None]), 0.0)
    request_total = jnp.sum(coef * page_total[:, None], axis=0)
    request_accum = jnp.einsum("prhg,phgd->rhgd", coef, page_accum)
    return (request_max, request_total, request_accum)


def finish_context(parts, local_queries, local_entries):
    entry_count = local_queries.shape[0]
    key_value_width = KEY_VALUE_HEADS * HEAD_SIZE
    query_groups = QUERY_HEADS // KEY_VALUE_HEADS
    query_vector = local_queries.reshape(entry_count, KEY_VALUE_HEADS, query_groups, HEAD_SIZE)
    token_key = local_entries[:, :key_value_width].reshape(entry_count, KEY_VALUE_HEADS, HEAD_SIZE)
    token_value = (
        local_entries[:, key_value_width:]
        .reshape(entry_count, KEY_VALUE_HEADS, 1, HEAD_SIZE)
        .astype(jnp.float32)
    )
    token_value = jnp.broadcast_to(
        token_value, (entry_count, KEY_VALUE_HEADS, query_groups, HEAD_SIZE)
    ).reshape(entry_count, QUERY_HEADS, HEAD_SIZE)
    own_score = jnp.einsum(
        "rhgd,rhd->rhg", query_vector, token_key, preferred_element_type=jnp.float32
    ).reshape(entry_count, QUERY_HEADS) * (1.0 / math.sqrt(HEAD_SIZE))
    parts = parts.astype(jnp.float32)
    heads = QUERY_HEADS
    part_max = parts[..., :heads] + parts[..., heads : 2 * heads]
    part_total = parts[..., 2 * heads : 3 * heads]
    part_accum = parts[..., 3 * heads :].reshape(parts.shape[:2] + (heads, HEAD_SIZE))
    joined = jnp.maximum(jnp.max(part_max, axis=1), own_score)
    coef = jnp.exp(part_max - joined[:, None])
    own_weight = jnp.exp(own_score - joined)
    totals = jnp.sum(coef * part_total, axis=1) + own_weight
    accum = jnp.sum(coef[..., None] * part_accum, axis=1) + own_weight[..., None] * token_value
    return (
        (accum / totals[..., None])
        .reshape(entry_count, QUERY_HEADS * HEAD_SIZE)
        .astype(jnp.bfloat16)
    )


def local(
    stream,
    queries,
    fresh_entries,
    paged_store_cache,
    page_table,
    cache_length,
    out_proj,
    norm_gain,
    router,
    routes,
    gate_up,
    down_proj,
):
    tensor_count = lax.axis_size(TENSOR)
    my_index = lax.axis_index(TENSOR)
    dec_rows = queries.shape[0]
    query_all = gather_nested(queries)
    request_max, request_total, request_accum = local_parts(
        query_all, paged_store_cache, page_table, cache_length, my_index
    )
    max_high = lax.reduce_precision(request_max, exponent_bits=8, mantissa_bits=7)
    max_low = lax.reduce_precision(request_max - max_high, exponent_bits=8, mantissa_bits=7)
    rebase = jnp.where(
        request_max > 0.5 * NEG_FILL, jnp.exp(request_max - (max_high + max_low)), 0.0
    )
    rows_out = request_max.shape[0]
    packed = jnp.concatenate(
        (
            max_high.reshape(rows_out, QUERY_HEADS),
            max_low.reshape(rows_out, QUERY_HEADS),
            (request_total * rebase).reshape(rows_out, QUERY_HEADS),
            (request_accum * rebase[..., None]).reshape(rows_out, QUERY_HEADS * HEAD_SIZE),
        ),
        axis=-1,
    ).astype(jnp.bfloat16)
    packed = packed.reshape(tensor_count, dec_rows, -1)
    parts = lax.all_to_all(packed, TENSOR, split_axis=0, concat_axis=0, tiled=True)
    parts = jnp.swapaxes(parts, 0, 1)
    context = finish_context(parts, queries, fresh_entries)
    context_all = gather_nested(context)
    projected = jnp.dot(context_all, out_proj, preferred_element_type=jnp.float32)
    column_block = projected.shape[1]
    arrived = lax.all_to_all(
        projected.reshape(tensor_count, dec_rows, column_block),
        TENSOR,
        split_axis=0,
        concat_axis=2,
        tiled=True,
    )
    widened = stream.astype(jnp.float32)
    widened = widened.at[:dec_rows].add(arrived[0])
    resid = lax.optimization_barrier(widened.astype(jnp.bfloat16))
    widened = resid.astype(jnp.float32)
    inverse = lax.rsqrt(jnp.mean(widened * widened, axis=-1, keepdims=True) + EPSILON)
    normed = (widened * inverse * norm_gain.astype(jnp.float32)).astype(jnp.bfloat16)
    logits = jnp.dot(normed, router, preferred_element_type=jnp.float32)
    chosen = jnp.take_along_axis(logits, routes, axis=1)
    gate_probs = jax.nn.softmax(chosen, axis=-1)
    expert_count = tensor_count // GROUP
    expert_ids = jnp.arange(expert_count, dtype=jnp.int32)
    matched = routes[:, :, None] == expert_ids[None, None, :]
    routed = jnp.any(matched, axis=1)
    gate_weight = jnp.sum(jnp.where(matched, gate_probs[:, :, None], 0.0), axis=1)
    routed_count = routed.astype(jnp.int32)
    ranking = jnp.cumsum(routed_count, axis=0) - routed_count
    slot_ids = jnp.arange(CAP, dtype=jnp.int32)
    selector = routed.T[None, :, :] & (ranking.T[None, :, :] == slot_ids[:, None, None])
    slot_rows = jnp.einsum(
        "cei,id->ced", selector.astype(jnp.bfloat16), normed, preferred_element_type=jnp.float32
    ).astype(jnp.bfloat16)
    landed = lax.all_to_all(slot_rows, EXPERT_AXES, split_axis=1, concat_axis=1, tiled=True)
    z_low = lax.axis_size("zl")
    own_rows = gather_axis(landed[None], "zl", z_low)
    swap = [(0, 1), (1, 0)]
    partner_rows = lax.ppermute(own_rows, "c", swap)

    def expert_partial(rows):
        flat_rows = rows.reshape(-1, rows.shape[-1])
        contract_last = (((1,), (1,)), ((), ()))
        gate_part = lax.dot_general(
            flat_rows, gate_up[0], contract_last, preferred_element_type=jnp.float32
        )
        upward = lax.dot_general(
            flat_rows, gate_up[1], contract_last, preferred_element_type=jnp.float32
        )
        active = (jax.nn.silu(gate_part) * upward).astype(jnp.bfloat16)
        partial_value = jnp.dot(active, down_proj, preferred_element_type=jnp.float32)
        return partial_value.astype(jnp.bfloat16).astype(jnp.float32).reshape(rows.shape)

    own_partial = expert_partial(own_rows)
    partner_partial = expert_partial(partner_rows)
    core_sum = own_partial + lax.ppermute(partner_partial, "c", swap)
    slice_sum = scatter_sum_axis(core_sum.astype(jnp.bfloat16), "zl", z_low)
    expert_out = lax.all_to_all(
        slice_sum.astype(jnp.bfloat16), EXPERT_AXES, split_axis=1, concat_axis=1, tiled=True
    ).astype(jnp.float32)
    weighted = selector.astype(jnp.float32) * gate_weight.T[None, :, :]
    routed_sum = jnp.einsum("cei,ced->id", weighted, expert_out)
    return (widened + routed_sum).astype(jnp.bfloat16)


def physical_mesh(mesh):
    dp_count, tensor_count = mesh.devices.shape
    z_count = tensor_count // 2 // 4
    z_low = GROUP // 2
    shape = (dp_count, 4, z_count // z_low, z_low, 2)
    return Mesh(np.asarray(mesh.devices).reshape(shape), ("dp",) + TENSOR)


def solution(mesh):
    mesh = physical_mesh(mesh)
    rows = ("dp",) + TENSOR
    placed = (
        P(rows, None),
        P(rows, None),
        P(rows, None),
        P(rows, None, None, None),
        P("dp", None),
        P("dp"),
        P(None, TENSOR),
        P(),
        P(),
        P(rows, None),
        P(None, TENSOR, None),
        P(TENSOR, None),
    )
    return jax.shard_map(
        local, mesh=mesh, in_specs=placed, out_specs=P(rows, None), check_vma=False
    )
```
